32 devices in a mesh: seq: 8 (over y, x, core), head: 4 (over z).
Axes of the slice: x: 2, y: 2, z: 4, core: 2. Of those that a mesh axis runs over, the one named last changes fastest.
Arguments:
- tokens: bfloat16 [16384, 768], P(('seq', 'head')), may hold values from -16 to 16
- w_qkv: bfloat16 [768, 3, 768], replicated, may hold values from -0.21875 to 0.21875
- w_out: bfloat16 [768, 768], replicated, may hold values from -0.21875 to 0.21875
- neighbours: int32 [128, 12], P('seq'), may hold values from 0 to 127, as said below
- near_count: int32 [128], P('seq'), may hold values from 1 to 12
- anchors: int32 [128, 8], P('seq'), may hold values from 0 to 112, as said below
Outputs:
- mixed_out: bfloat16 [16384, 768], P(('seq', 'head'))
The draws below stay inside these ranges and needn't reach their ends.
Inputs may be any that keep to these rules, and one draw needn't show every extreme that they name: `neighbours`: entry 0 of row b is b itself; the entries of a row are distinct and lie within 32 blocks of b. `anchors`: every entry is a multiple of 16; the entries of a row are distinct.
All inputs are finite; a program needn't handle non-finite values.
Results may differ from the reference program's by a relative error of at most 0.006.
The reference program's roundings to bfloat16 on the way (of `projected`, `weights` and `attended`) count: a program that leaves them out, or rounds other values in their place, can miss the bound.
Values may be sent and summed in bfloat16 or wider, within the bound.
No kernel may reach another device: no remote copies, remote signals or barrier semaphores. Data moves between devices by JAX's collectives and lax.ppermute only.
A program may use at most 128 MiB of HBM per device.

```python
import jax
import jax.numpy as jnp
from jax import lax

D = 768
HEADS = 12
HDIM = 64
BLK = 128
NEIGH = 12
ANCH = 8
TOKENS = 16384
BPD = 16
NB = 128


def draw_tokens(key, part):
    values = jnp.clip(jax.random.normal(key, (TOKENS, D), jnp.float32), -4.0, 4.0)
    return values.astype(jnp.bfloat16)


def draw_neighbours(key, part):
    reach = 2 * BPD
    span = 2 * reach
    offsets = jnp.concatenate([jnp.arange(-reach, 0), jnp.arange(1, reach + 1)]).astype(jnp.int32)
    targets = jnp.arange(NB, dtype=jnp.int32)[:, None] + offsets[None, :]
    scores = jax.random.randint(key, (NB, span), 0, 65536, dtype=jnp.int32) * span + jnp.arange(span, dtype=jnp.int32)[None, :]
    outside = (targets < 0) | (targets >= NB)
    scores = jnp.where(outside, scores + 16777216, scores)
    order = jnp.argsort(scores, axis=1)
    picked = jnp.take_along_axis(targets, order[:, :NEIGH - 1], axis=1)
    return jnp.concatenate([jnp.arange(NB, dtype=jnp.int32)[:, None], picked], axis=1).astype(jnp.int32)


def draw_near_count(key, part):
    counts = jax.random.randint(key, (NB,), 1, NEIGH + 1, dtype=jnp.int32)
    counts = counts.at[0].set(NEIGH)
    counts = counts.at[NB - 1].set(1)
    return counts.astype(jnp.int32)


def draw_anchors(key, part):
    owners = NB // BPD
    scores = jax.random.randint(key, (NB, owners), 0, 65536, dtype=jnp.int32) * owners + jnp.arange(owners, dtype=jnp.int32)[None, :]
    scores = scores.at[0, owners - 1].set(-1)
    scores = scores.at[1, 0].set(-1)
    order = jnp.argsort(scores, axis=1)
    return (order[:, :ANCH] * BPD).astype(jnp.int32)


def noise(own_key, shape, deviation, most, kind=jnp.bfloat16):
    return jnp.clip(deviation * jax.random.normal(own_key, shape, jnp.float32), -most, most).astype(kind)


def setup_inputs(seed: int = 0) -> dict:
    key_list = jax.random.split(jax.random.key(seed), 7)
    tokens = draw_tokens(jax.random.fold_in(key_list[6], 71), 0)
    w_qkv = noise(key_list[1], (D, 3, D), D ** -0.5, 0.21875)
    w_out = noise(key_list[2], (D, D), D ** -0.5, 0.21875)
    neighbours = draw_neighbours(jax.random.fold_in(key_list[6], 71), 0)
    near_count = draw_near_count(jax.random.fold_in(key_list[6], 71), 0)
    anchors = draw_anchors(jax.random.fold_in(key_list[6], 71), 0)
    return dict(tokens=tokens, w_qkv=w_qkv, w_out=w_out, neighbours=neighbours, near_count=near_count, anchors=anchors)


def reference(tokens, w_qkv, w_out, neighbours, near_count, anchors):
    projected = jnp.dot(tokens, w_qkv.reshape(D, 3 * D), preferred_element_type=jnp.float32).astype(jnp.bfloat16)
    projected = projected.reshape(TOKENS, 3, HEADS, HDIM)
    block_count = TOKENS // BLK
    queries = projected[:, 0].reshape(block_count, BLK, HEADS, HDIM)
    key_blocks = projected[:, 1].reshape(block_count, BLK, HEADS, HDIM)
    value_blocks = projected[:, 2].reshape(block_count, BLK, HEADS, HDIM)
    scale = HDIM ** -0.5

    def one_block(inputs):
        query_block, near_rows, used_count, anchor_rows = inputs
        chosen = jnp.concatenate([near_rows, anchor_rows]).astype(jnp.int32)
        near_used = jnp.arange(NEIGH) < used_count
        repeated = jnp.any((anchor_rows[:, None] == near_rows[None, :]) & near_used[None, :], axis=1)
        usable = jnp.concatenate([near_used, jnp.logical_not(repeated)])
        allowed = jnp.repeat(usable, BLK)
        key_part = jnp.take(key_blocks, chosen, axis=0).reshape(-1, HEADS, HDIM).astype(jnp.float32)
        value_part = jnp.take(value_blocks, chosen, axis=0).reshape(-1, HEADS, HDIM).astype(jnp.float32)
        scores = jnp.einsum('qhd,khd->hqk', query_block.astype(jnp.float32), key_part) * scale
        scores = jnp.where(allowed[None, None, :], scores, -1e30)
        peak = jnp.max(scores, axis=-1, keepdims=True)
        expterm = jnp.where(allowed[None, None, :], jnp.exp(scores - peak), 0.0)
        totals = jnp.sum(expterm, axis=-1)
        weights = lax.optimization_barrier(expterm.astype(jnp.bfloat16)).astype(jnp.float32)
        summed = jnp.einsum('hqk,khd->qhd', weights, value_part)
        attended = summed / jnp.transpose(totals)[:, :, None]
        return attended.astype(jnp.bfloat16).reshape(BLK, D)

    attended = lax.map(one_block, (queries, neighbours, near_count, anchors)).reshape(TOKENS, D)
    return jnp.dot(attended, w_out, preferred_element_type=jnp.float32).astype(jnp.bfloat16)
```

```python
import functools

import jax
import jax.numpy as jnp
from jax import lax
from jax.experimental import pallas as pl
from jax.experimental.pallas import tpu as pltpu
from jax.sharding import PartitionSpec as P

D = 768
HDIM = 64
BLK = 128


def shifted(x, axis, by):
    size = lax.axis_size(axis)
    pairs = [(i, i + by) for i in range(size) if 0 <= i + by < size]
    return lax.ppermute(x, axis, pairs)


def gather_all(x, axis):
    size = lax.axis_size(axis)
    rank = lax.axis_index(axis)
    held = x[None]
    step = 1
    while step < size:
        pairs = [(i, (i + step) % size) for i in range(size)]
        got = lax.ppermute(held, axis, pairs)
        held = jnp.concatenate([got, held], axis=0)
        step *= 2
    return held


def attention_kernel(near_idx, anch_idx, valid, q_ref, win_ref, anc_ref, o_ref,
                     sc_ref, m_ref, l_ref, acc_ref, *, heads, neigh, anch, scale):
    b = pl.program_id(0)
    width = heads * HDIM
    for h in range(heads):
        qcols = slice(h * HDIM, (h + 1) * HDIM)
        kcols = pl.ds(h * HDIM, HDIM)
        vcols = pl.ds(width + h * HDIM, HDIM)
        qh = q_ref[0, :, qcols]

        def scores_of(src, row):
            k = src[row, :, kcols]
            return lax.dot_general(qh, k, (((1,), (1,)), ((), ())),
                                   preferred_element_type=jnp.float32)

        first = scores_of(win_ref, near_idx[b, 0])
        sc_ref[0] = first
        m_ref[...] = first

        def near_pass1(j, carry):
            @pl.when(valid[b, j] != 0)
            def _():
                s = scores_of(win_ref, near_idx[b, j])
                sc_ref[j] = s
                m_ref[...] = jnp.maximum(m_ref[...], s)
            return carry

        def anch_pass1(j, carry):
            @pl.when(valid[b, neigh + j] != 0)
            def _():
                s = scores_of(anc_ref, anch_idx[b, j])
                sc_ref[neigh + j] = s
                m_ref[...] = jnp.maximum(m_ref[...], s)
            return carry

        lax.fori_loop(1, neigh, near_pass1, 0)
        lax.fori_loop(0, anch, anch_pass1, 0)
        peak = jnp.max(m_ref[...], axis=-1, keepdims=True)
        l_ref[...] = jnp.zeros_like(l_ref)
        acc_ref[...] = jnp.zeros_like(acc_ref)

        def accumulate(slot, src, row):
            e = jnp.exp((sc_ref[slot] - peak) * scale)
            l_ref[...] += e
            v = src[row, :, vcols]
            acc_ref[...] += jnp.dot(e.astype(jnp.bfloat16), v,
                                    preferred_element_type=jnp.float32)

        def near_pass2(j, carry):
            @pl.when(valid[b, j] != 0)
            def _():
                accumulate(j, win_ref, near_idx[b, j])
            return carry

        def anch_pass2(j, carry):
            @pl.when(valid[b, neigh + j] != 0)
            def _():
                accumulate(neigh + j, anc_ref, anch_idx[b, j])
            return carry

        lax.fori_loop(0, neigh, near_pass2, 0)
        lax.fori_loop(0, anch, anch_pass2, 0)
        totals = jnp.sum(l_ref[...], axis=-1, keepdims=True)
        o_ref[0, :, qcols] = (acc_ref[...] / totals).astype(o_ref.dtype)


def attention(queries, window, anchor_table, near_idx, anch_idx, valid):
    block_count, _, width = queries.shape
    heads = width // HDIM
    neigh = near_idx.shape[1]
    anch = anch_idx.shape[1]
    kernel = functools.partial(attention_kernel, heads=heads, neigh=neigh, anch=anch,
                               scale=HDIM ** (-0.5))
    whole = pl.BlockSpec(memory_space=pltpu.VMEM)
    return pl.pallas_call(
        kernel,
        out_shape=jax.ShapeDtypeStruct(queries.shape, jnp.bfloat16),
        grid_spec=pltpu.PrefetchScalarGridSpec(
            num_scalar_prefetch=3,
            grid=(block_count,),
            in_specs=[
                pl.BlockSpec((1, BLK, width), lambda b, *_: (b, 0, 0)),
                whole,
                whole,
            ],
            out_specs=pl.BlockSpec((1, BLK, width), lambda b, *_: (b, 0, 0)),
            scratch_shapes=[
                pltpu.VMEM((neigh + anch, BLK, BLK), jnp.float32),
                pltpu.VMEM((BLK, BLK), jnp.float32),
                pltpu.VMEM((BLK, BLK), jnp.float32),
                pltpu.VMEM((BLK, HDIM), jnp.float32),
            ],
        ),
        compiler_params=pltpu.CompilerParams(vmem_limit_bytes=60 * 1024 * 1024),
    )(near_idx, anch_idx, valid, queries, window, anchor_table)


def shards(tokens, w_qkv, w_out, neighbours, near_count, anchors):
    gathered = lax.all_gather(tokens, "head", axis=0, tiled=True)
    head_count = lax.axis_size("head")
    head_rank = lax.axis_index("head")
    width_here = D // head_count
    row_count = gathered.shape[0]
    block_count = row_count // BLK
    neigh = neighbours.shape[1]
    col_start = head_rank * width_here
    query_cols = lax.dynamic_slice_in_dim(w_qkv[:, 0], col_start, width_here, 1)
    key_cols = lax.dynamic_slice_in_dim(w_qkv[:, 1], col_start, width_here, 1)
    value_cols = lax.dynamic_slice_in_dim(w_qkv[:, 2], col_start, width_here, 1)
    own_weights = jnp.concatenate([query_cols, key_cols, value_cols], axis=1)
    projected = jnp.dot(gathered, own_weights, preferred_element_type=jnp.float32).astype(
        jnp.bfloat16
    )
    queries = projected[:, :width_here].reshape(block_count, BLK, width_here)
    keyval = projected[:, width_here:]
    seq_count = lax.axis_size("seq")
    seq_rank = lax.axis_index("seq")
    beside = {}
    for offset in (2, 1, -1, -2):
        beside[offset] = shifted(keyval, "seq", offset)
    window = jnp.concatenate([beside[2], beside[1], keyval, beside[-1], beside[-2]], axis=0)
    window = window.reshape(5 * block_count, BLK, 2 * width_here)
    anchor_table = gather_all(keyval[:BLK].reshape(BLK, 2 * width_here), "seq")
    held_count = anchor_table.shape[0]
    first_block = (seq_rank - 2) * block_count

    near_idx = jnp.clip(neighbours - first_block, 0, 5 * block_count - 1).astype(jnp.int32)
    owner = jnp.clip(anchors // block_count, 0, seq_count - 1)
    anch_idx = ((owner - seq_rank + held_count - 1) % seq_count).astype(jnp.int32)
    near_used = jnp.arange(neigh)[None, :] < near_count[:, None]
    repeated = jnp.any(
        (anchors[:, :, None] == neighbours[:, None, :]) & near_used[:, None, :], axis=2
    )
    valid = jnp.concatenate([near_used, jnp.logical_not(repeated)], axis=1).astype(jnp.int32)

    attended = attention(queries, window, anchor_table, near_idx, anch_idx, valid)
    attended = attended.reshape(row_count, width_here)
    mine = lax.all_to_all(attended, "head", 0, 1, tiled=True)
    mixed_out = jnp.dot(mine, w_out, preferred_element_type=jnp.float32).astype(jnp.bfloat16)
    return mixed_out


def solution(mesh):
    placed = (P(("seq", "head"), None), P(), P(), P("seq", None), P("seq"), P("seq", None))
    return jax.shard_map(
        shards, mesh=mesh, in_specs=placed, out_specs=P(("seq", "head"), None), check_vma=False
    )
```

```python
import functools

import jax
import jax.numpy as jnp
from jax import lax
from jax.experimental import pallas as pl
from jax.experimental.pallas import tpu as pltpu
from jax.sharding import PartitionSpec as P

D = 768
HDIM = 64
BLK = 128


def shifted(x, axis, by):
    size = lax.axis_size(axis)
    pairs = [(i, i + by) for i in range(size) if 0 <= i + by < size]
    return lax.ppermute(x, axis, pairs)


def gather_all(x, axis):
    size = lax.axis_size(axis)
    rank = lax.axis_index(axis)
    held = x[None]
    step = 1
    while step < size:
        pairs = [(i, (i + step) % size) for i in range(size)]
        got = lax.ppermute(held, axis, pairs)
        held = jnp.concatenate([got, held], axis=0)
        step *= 2
    return held


def attention_kernel(count, from_anchor, rows, q_ref, win_ref, anc_ref, o_ref,
                     kv_ref, sc_ref, m_ref, l_ref, acc_ref, *, heads, group, groups, scale):
    b = pl.program_id(0)
    width = heads * HDIM
    used = count[b]
    span = group * BLK

    @pl.when(b == 0)
    def _():
        kv_ref[...] = jnp.zeros_like(kv_ref)

    def fetch(j, carry):
        dst = pl.ds(pl.multiple_of(j * BLK, BLK), BLK)
        row = rows[b, j]

        @pl.when(from_anchor[b, j] == 0)
        def _():
            kv_ref[dst, :] = win_ref[row]

        @pl.when(from_anchor[b, j] != 0)
        def _():
            kv_ref[dst, :] = anc_ref[row]

        return carry

    lax.fori_loop(0, used, fetch, 0)
    limit = used * BLK
    for h in range(heads):
        qcols = slice(h * HDIM, (h + 1) * HDIM)
        kcols = slice(h * HDIM, (h + 1) * HDIM)
        vcols = slice(width + h * HDIM, width + (h + 1) * HDIM)
        qh = q_ref[0, :, qcols]

        def scores_of(c):
            k = kv_ref[c * span:(c + 1) * span, kcols]
            s = lax.dot_general(qh, k, (((1,), (1,)), ((), ())),
                                preferred_element_type=jnp.float32)
            col = c * span + lax.broadcasted_iota(jnp.int32, s.shape, 1)
            return jnp.where(col < limit, s, -jnp.inf)

        first = scores_of(0)
        sc_ref[:, 0:span] = first
        m_ref[...] = first
        for c in range(1, groups):
            @pl.when(c * group < used)
            def _():
                s = scores_of(c)
                sc_ref[:, c * span:(c + 1) * span] = s
                m_ref[...] = jnp.maximum(m_ref[...], s)

        peak = jnp.max(m_ref[...], axis=-1, keepdims=True)
        l_ref[...] = jnp.zeros_like(l_ref)
        acc_ref[...] = jnp.zeros_like(acc_ref)
        for c in range(groups):
            @pl.when(c * group < used)
            def _():
                e = jnp.exp((sc_ref[:, c * span:(c + 1) * span] - peak) * scale)
                l_ref[...] += e
                v = kv_ref[c * span:(c + 1) * span, vcols]
                acc_ref[...] += jnp.dot(e.astype(jnp.bfloat16), v,
                                        preferred_element_type=jnp.float32)

        totals = jnp.sum(l_ref[...], axis=-1, keepdims=True)
        o_ref[0, :, qcols] = (acc_ref[...] / totals).astype(o_ref.dtype)


def attention(queries, window, anchor_table, count, from_anchor, rows):
    block_count, _, width = queries.shape
    heads = width // HDIM
    slots = rows.shape[1]
    group = 4
    groups = -(-slots // group)
    kernel = functools.partial(attention_kernel, heads=heads, group=group, groups=groups,
                               scale=HDIM ** (-0.5))
    whole = pl.BlockSpec(memory_space=pltpu.VMEM)
    return pl.pallas_call(
        kernel,
        out_shape=jax.ShapeDtypeStruct(queries.shape, jnp.bfloat16),
        grid_spec=pltpu.PrefetchScalarGridSpec(
            num_scalar_prefetch=3,
            grid=(block_count,),
            in_specs=[
                pl.BlockSpec((1, BLK, width), lambda b, *_: (b, 0, 0)),
                whole,
                whole,
            ],
            out_specs=pl.BlockSpec((1, BLK, width), lambda b, *_: (b, 0, 0)),
            scratch_shapes=[
                pltpu.VMEM((groups * group * BLK, 2 * width), jnp.bfloat16),
                pltpu.VMEM((BLK, groups * group * BLK), jnp.float32),
                pltpu.VMEM((BLK, group * BLK), jnp.float32),
                pltpu.VMEM((BLK, group * BLK), jnp.float32),
                pltpu.VMEM((BLK, HDIM), jnp.float32),
            ],
        ),
        compiler_params=pltpu.CompilerParams(vmem_limit_bytes=60 * 1024 * 1024),
    )(count, from_anchor, rows, queries, window, anchor_table)


def shards(tokens, w_qkv, w_out, neighbours, near_count, anchors):
    gathered = lax.all_gather(tokens, "head", axis=0, tiled=True)
    head_count = lax.axis_size("head")
    head_rank = lax.axis_index("head")
    width_here = D // head_count
    row_count = gathered.shape[0]
    block_count = row_count // BLK
    neigh = neighbours.shape[1]
    col_start = head_rank * width_here
    query_cols = lax.dynamic_slice_in_dim(w_qkv[:, 0], col_start, width_here, 1)
    key_cols = lax.dynamic_slice_in_dim(w_qkv[:, 1], col_start, width_here, 1)
    value_cols = lax.dynamic_slice_in_dim(w_qkv[:, 2], col_start, width_here, 1)
    own_weights = jnp.concatenate([query_cols, key_cols, value_cols], axis=1)
    projected = jnp.dot(gathered, own_weights, preferred_element_type=jnp.float32).astype(
        jnp.bfloat16
    )
    queries = projected[:, :width_here].reshape(block_count, BLK, width_here)
    keyval = projected[:, width_here:]
    seq_count = lax.axis_size("seq")
    seq_rank = lax.axis_index("seq")
    beside = {}
    for offset in (2, 1, -1, -2):
        beside[offset] = shifted(keyval, "seq", offset)
    window = jnp.concatenate([beside[2], beside[1], keyval, beside[-1], beside[-2]], axis=0)
    window = window.reshape(5 * block_count, BLK, 2 * width_here)
    anchor_table = gather_all(keyval[:BLK].reshape(BLK, 2 * width_here), "seq")
    held_count = anchor_table.shape[0]
    first_block = (seq_rank - 2) * block_count

    near_idx = jnp.clip(neighbours - first_block, 0, 5 * block_count - 1).astype(jnp.int32)
    owner = jnp.clip(anchors // block_count, 0, seq_count - 1)
    anch_idx = ((owner - seq_rank + held_count - 1) % seq_count).astype(jnp.int32)
    near_used = jnp.arange(neigh)[None, :] < near_count[:, None]
    repeated = jnp.any(
        (anchors[:, :, None] == neighbours[:, None, :]) & near_used[:, None, :], axis=2
    )
    valid = jnp.concatenate([near_used, jnp.logical_not(repeated)], axis=1)
    order = jnp.argsort(jnp.logical_not(valid).astype(jnp.int32), axis=1, stable=True)
    every_row = jnp.concatenate([near_idx, anch_idx], axis=1)
    rows = jnp.take_along_axis(every_row, order, axis=1).astype(jnp.int32)
    from_anchor = (order >= neigh).astype(jnp.int32)
    count = jnp.sum(valid.astype(jnp.int32), axis=1).astype(jnp.int32)

    attended = attention(queries, window, anchor_table, count, from_anchor, rows)
    attended = attended.reshape(row_count, width_here)
    mine = lax.all_to_all(attended, "head", 0, 1, tiled=True)
    mixed_out = jnp.dot(mine, w_out, preferred_element_type=jnp.float32).astype(jnp.bfloat16)
    return mixed_out


def solution(mesh):
    placed = (P(("seq", "head"), None), P(), P(), P("seq", None), P("seq"), P("seq", None))
    return jax.shard_map(
        shards, mesh=mesh, in_specs=placed, out_specs=P(("seq", "head"), None), check_vma=False
    )
```

```python
import functools

import jax
import jax.numpy as jnp
from jax import lax
from jax.experimental import pallas as pl
from jax.experimental.pallas import tpu as pltpu
from jax.sharding import PartitionSpec as P

D = 768
HDIM = 64
BLK = 128


def shifted(x, axis, by):
    size = lax.axis_size(axis)
    pairs = [(i, i + by) for i in range(size) if 0 <= i + by < size]
    return lax.ppermute(x, axis, pairs)


def gather_all(x, axis):
    size = lax.axis_size(axis)
    rank = lax.axis_index(axis)
    held = x[None]
    step = 1
    while step < size:
        pairs = [(i, (i + step) % size) for i in range(size)]
        got = lax.ppermute(held, axis, pairs)
        held = jnp.concatenate([got, held], axis=0)
        step *= 2
    return held


def attention_kernel(count, from_anchor, rows, q_ref, kwin_ref, vwin_ref, kanc_ref, vanc_ref,
                     o_ref, kt_ref, v_ref, sc_ref, m_ref, l_ref, acc_ref,
                     *, heads, group, groups, scale):
    b = pl.program_id(0)
    used = count[b]
    span = group * BLK

    @pl.when(b == 0)
    def _():
        kt_ref[...] = jnp.zeros_like(kt_ref)
        v_ref[...] = jnp.zeros_like(v_ref)

    def fetch(j, carry):
        at = pl.multiple_of(j * BLK, BLK)
        row = rows[b, j]

        @pl.when(from_anchor[b, j] == 0)
        def _():
            kt_ref[:, pl.ds(at, BLK)] = kwin_ref[row]
            v_ref[pl.ds(at, BLK), :] = vwin_ref[row]

        @pl.when(from_anchor[b, j] != 0)
        def _():
            kt_ref[:, pl.ds(at, BLK)] = kanc_ref[row]
            v_ref[pl.ds(at, BLK), :] = vanc_ref[row]

        return carry

    lax.fori_loop(0, used, fetch, 0)
    limit = used * BLK
    lane = lax.broadcasted_iota(jnp.int32, (1, span), 1)
    for h in range(heads):
        cols = slice(h * HDIM, (h + 1) * HDIM)
        qh = (q_ref[0, :, cols].astype(jnp.float32) * scale).astype(jnp.bfloat16)

        def scores_of(c):
            s = jnp.dot(qh, kt_ref[cols, c * span:(c + 1) * span],
                        preferred_element_type=jnp.float32)
            bias = jnp.where(lane < limit - c * span, 0.0, -jnp.inf)
            return s + bias

        first = scores_of(0)
        sc_ref[:, 0:span] = first
        m_ref[...] = first
        for c in range(1, groups):
            @pl.when(c * group < used)
            def _():
                s = scores_of(c)
                sc_ref[:, c * span:(c + 1) * span] = s
                m_ref[...] = jnp.maximum(m_ref[...], s)

        peak = jnp.max(m_ref[...], axis=-1, keepdims=True)
        l_ref[...] = jnp.zeros_like(l_ref)
        acc_ref[...] = jnp.zeros_like(acc_ref)
        for c in range(groups):
            @pl.when(c * group < used)
            def _():
                e = jnp.exp(sc_ref[:, c * span:(c + 1) * span] - peak)
                l_ref[...] += e
                acc_ref[...] += jnp.dot(e.astype(jnp.bfloat16),
                                        v_ref[c * span:(c + 1) * span, cols],
                                        preferred_element_type=jnp.float32)

        totals = jnp.sum(l_ref[...], axis=-1, keepdims=True)
        o_ref[0, :, cols] = (acc_ref[...] / totals).astype(o_ref.dtype)


def attention(queries, kwin, vwin, kanc, vanc, count, from_anchor, rows):
    block_count, _, width = queries.shape
    heads = width // HDIM
    slots = rows.shape[1]
    group = 4
    groups = -(-slots // group)
    kernel = functools.partial(attention_kernel, heads=heads, group=group, groups=groups,
                               scale=HDIM ** (-0.5))
    whole = pl.BlockSpec(memory_space=pltpu.VMEM)
    keys = groups * group * BLK
    return pl.pallas_call(
        kernel,
        out_shape=jax.ShapeDtypeStruct(queries.shape, jnp.bfloat16),
        grid_spec=pltpu.PrefetchScalarGridSpec(
            num_scalar_prefetch=3,
            grid=(block_count,),
            in_specs=[
                pl.BlockSpec((1, BLK, width), lambda b, *_: (b, 0, 0)),
                whole,
                whole,
                whole,
                whole,
            ],
            out_specs=pl.BlockSpec((1, BLK, width), lambda b, *_: (b, 0, 0)),
            scratch_shapes=[
                pltpu.VMEM((width, keys), jnp.bfloat16),
                pltpu.VMEM((keys, width), jnp.bfloat16),
                pltpu.VMEM((BLK, keys), jnp.float32),
                pltpu.VMEM((BLK, group * BLK), jnp.float32),
                pltpu.VMEM((BLK, group * BLK), jnp.float32),
                pltpu.VMEM((BLK, HDIM), jnp.float32),
            ],
        ),
        compiler_params=pltpu.CompilerParams(vmem_limit_bytes=60 * 1024 * 1024),
    )(count, from_anchor, rows, queries, kwin, vwin, kanc, vanc)


def shards(tokens, w_qkv, w_out, neighbours, near_count, anchors):
    gathered = lax.all_gather(tokens, "head", axis=0, tiled=True)
    head_count = lax.axis_size("head")
    head_rank = lax.axis_index("head")
    width_here = D // head_count
    row_count = gathered.shape[0]
    block_count = row_count // BLK
    neigh = neighbours.shape[1]
    col_start = head_rank * width_here
    query_cols = lax.dynamic_slice_in_dim(w_qkv[:, 0], col_start, width_here, 1)
    key_cols = lax.dynamic_slice_in_dim(w_qkv[:, 1], col_start, width_here, 1)
    value_cols = lax.dynamic_slice_in_dim(w_qkv[:, 2], col_start, width_here, 1)
    own_weights = jnp.concatenate([query_cols, key_cols, value_cols], axis=1)
    projected = jnp.dot(gathered, own_weights, preferred_element_type=jnp.float32).astype(
        jnp.bfloat16
    )
    queries = projected[:, :width_here].reshape(block_count, BLK, width_here)
    keys_t = jnp.transpose(
        projected[:, width_here:2 * width_here].reshape(block_count, BLK, width_here), (0, 2, 1)
    )
    values = projected[:, 2 * width_here:].reshape(block_count, BLK, width_here)
    seq_count = lax.axis_size("seq")
    seq_rank = lax.axis_index("seq")
    kparts, vparts = [], []
    for offset in (2, 1, 0, -1, -2):
        if offset == 0:
            kparts.append(keys_t)
            vparts.append(values)
        else:
            kparts.append(shifted(keys_t, "seq", offset))
            vparts.append(shifted(values, "seq", offset))
    kwin = jnp.concatenate(kparts, axis=0)
    vwin = jnp.concatenate(vparts, axis=0)
    kanc = gather_all(keys_t[0], "seq")
    vanc = gather_all(values[0], "seq")
    held_count = kanc.shape[0]
    first_block = (seq_rank - 2) * block_count

    near_idx = jnp.clip(neighbours - first_block, 0, 5 * block_count - 1).astype(jnp.int32)
    owner = jnp.clip(anchors // block_count, 0, seq_count - 1)
    anch_idx = ((owner - seq_rank + held_count - 1) % seq_count).astype(jnp.int32)
    near_used = jnp.arange(neigh)[None, :] < near_count[:, None]
    repeated = jnp.any(
        (anchors[:, :, None] == neighbours[:, None, :]) & near_used[:, None, :], axis=2
    )
    valid = jnp.concatenate([near_used, jnp.logical_not(repeated)], axis=1)
    order = jnp.argsort(jnp.logical_not(valid).astype(jnp.int32), axis=1, stable=True)
    every_row = jnp.concatenate([near_idx, anch_idx], axis=1)
    rows = jnp.take_along_axis(every_row, order, axis=1).astype(jnp.int32)
    from_anchor = (order >= neigh).astype(jnp.int32)
    count = jnp.sum(valid.astype(jnp.int32), axis=1).astype(jnp.int32)

    attended = attention(queries, kwin, vwin, kanc, vanc, count, from_anchor, rows)
    attended = attended.reshape(row_count, width_here)
    mine = lax.all_to_all(attended, "head", 0, 1, tiled=True)
    mixed_out = jnp.dot(mine, w_out, preferred_element_type=jnp.float32).astype(jnp.bfloat16)
    return mixed_out


def solution(mesh):
    placed = (P(("seq", "head"), None), P(), P(), P("seq", None), P("seq"), P("seq", None))
    return jax.shard_map(
        shards, mesh=mesh, in_specs=placed, out_specs=P(("seq", "head"), None), check_vma=False
    )
```

```python
import functools

import jax
import jax.numpy as jnp
from jax import lax
from jax.experimental import pallas as pl
from jax.experimental.pallas import tpu as pltpu
from jax.sharding import PartitionSpec as P

D = 768
HDIM = 64
BLK = 128


def shifted(x, axis, by):
    size = lax.axis_size(axis)
    pairs = [(i, i + by) for i in range(size) if 0 <= i + by < size]
    return lax.ppermute(x, axis, pairs)


def gather_all(x, axis):
    size = lax.axis_size(axis)
    rank = lax.axis_index(axis)
    held = x[None]
    step = 1
    while step < size:
        pairs = [(i, (i + step) % size) for i in range(size)]
        got = lax.ppermute(held, axis, pairs)
        held = jnp.concatenate([got, held], axis=0)
        step *= 2
    return held


def attention_kernel(count, source, rows, q_ref, *refs, heads, group, groups, scale):
    tables = refs[:6]
    o_ref, kt_ref, v_ref, sc_ref, m_ref, l_ref, acc_ref = refs[6:]
    b = pl.program_id(0)
    used = count[b]
    span = group * BLK

    @pl.when(b == 0)
    def _():
        kt_ref[...] = jnp.zeros_like(kt_ref)
        v_ref[...] = jnp.zeros_like(v_ref)

    def fetch(j, carry):
        at = pl.multiple_of(j * BLK, BLK)
        row = rows[b, j]

        for code in range(3):
            @pl.when(source[b, j] == code)
            def _():
                kt_ref[:, pl.ds(at, BLK)] = tables[2 * code][row]
                v_ref[pl.ds(at, BLK), :] = tables[2 * code + 1][row]

        return carry

    lax.fori_loop(0, used, fetch, 0)
    limit = used * BLK
    lane = lax.broadcasted_iota(jnp.int32, (1, span), 1)
    for h in range(heads):
        cols = slice(h * HDIM, (h + 1) * HDIM)
        qh = (q_ref[0, :, cols].astype(jnp.float32) * scale).astype(jnp.bfloat16)

        def scores_of(c):
            s = jnp.dot(qh, kt_ref[cols, c * span:(c + 1) * span],
                        preferred_element_type=jnp.float32)
            bias = jnp.where(lane < limit - c * span, 0.0, -jnp.inf)
            return s + bias

        first = scores_of(0)
        sc_ref[:, 0:span] = first
        m_ref[...] = first
        for c in range(1, groups):
            @pl.when(c * group < used)
            def _():
                s = scores_of(c)
                sc_ref[:, c * span:(c + 1) * span] = s
                m_ref[...] = jnp.maximum(m_ref[...], s)

        peak = jnp.max(m_ref[...], axis=-1, keepdims=True)
        l_ref[...] = jnp.zeros_like(l_ref)
        acc_ref[...] = jnp.zeros_like(acc_ref)
        for c in range(groups):
            @pl.when(c * group < used)
            def _():
                e = jnp.exp(sc_ref[:, c * span:(c + 1) * span] - peak)
                l_ref[...] += e
                acc_ref[...] += jnp.dot(e.astype(jnp.bfloat16),
                                        v_ref[c * span:(c + 1) * span, cols],
                                        preferred_element_type=jnp.float32)

        totals = jnp.sum(l_ref[...], axis=-1, keepdims=True)
        o_ref[0, :, cols] = (acc_ref[...] / totals).astype(o_ref.dtype)


def attention(queries, tables, count, source, rows):
    block_count, _, width = queries.shape
    heads = width // HDIM
    slots = rows.shape[1]
    group = 2
    groups = -(-slots // group)
    kernel = functools.partial(attention_kernel, heads=heads, group=group, groups=groups,
                               scale=HDIM ** (-0.5))
    whole = pl.BlockSpec(memory_space=pltpu.VMEM)
    keys = groups * group * BLK
    return pl.pallas_call(
        kernel,
        out_shape=jax.ShapeDtypeStruct(queries.shape, jnp.bfloat16),
        grid_spec=pltpu.PrefetchScalarGridSpec(
            num_scalar_prefetch=3,
            grid=(block_count,),
            in_specs=[
                pl.BlockSpec((1, BLK, width), lambda b, *_: (b, 0, 0)),
            ] + [whole] * len(tables),
            out_specs=pl.BlockSpec((1, BLK, width), lambda b, *_: (b, 0, 0)),
            scratch_shapes=[
                pltpu.VMEM((width, keys), jnp.bfloat16),
                pltpu.VMEM((keys, width), jnp.bfloat16),
                pltpu.VMEM((BLK, keys), jnp.float32),
                pltpu.VMEM((BLK, group * BLK), jnp.float32),
                pltpu.VMEM((BLK, group * BLK), jnp.float32),
                pltpu.VMEM((BLK, HDIM), jnp.float32),
            ],
        ),
        compiler_params=pltpu.CompilerParams(vmem_limit_bytes=60 * 1024 * 1024),
    )(count, source, rows, queries, *tables)


def split_kv(projected, width, block_count):
    keys_t = jnp.transpose(
        projected[:, width:2 * width].reshape(block_count, BLK, width), (0, 2, 1)
    )
    values = projected[:, 2 * width:].reshape(block_count, BLK, width)
    return keys_t, values


def window_of(x):
    parts = []
    for offset in (2, 1, 0, -1, -2):
        parts.append(x if offset == 0 else shifted(x, "seq", offset))
    return jnp.concatenate(parts, axis=0)


def shards(tokens, w_qkv, w_out, neighbours, near_count, anchors):
    head_count = lax.axis_size("head")
    head_rank = lax.axis_index("head")
    width_here = D // head_count
    own_rows = tokens.shape[0]
    own_blocks = own_rows // BLK
    row_count = own_rows * head_count
    block_count = row_count // BLK
    neigh = neighbours.shape[1]
    col_start = head_rank * width_here
    query_cols = lax.dynamic_slice_in_dim(w_qkv[:, 0], col_start, width_here, 1)
    key_cols = lax.dynamic_slice_in_dim(w_qkv[:, 1], col_start, width_here, 1)
    value_cols = lax.dynamic_slice_in_dim(w_qkv[:, 2], col_start, width_here, 1)
    own_weights = jnp.concatenate([query_cols, key_cols, value_cols], axis=1)

    own_proj = jnp.dot(tokens, own_weights, preferred_element_type=jnp.float32).astype(
        jnp.bfloat16
    )
    k_own, v_own = split_kv(own_proj, width_here, own_blocks)
    ka, va = window_of(k_own), window_of(v_own)

    gathered = lax.all_gather(tokens, "head", axis=0, tiled=True)
    projected = jnp.dot(gathered, own_weights, preferred_element_type=jnp.float32).astype(
        jnp.bfloat16
    )
    queries = projected[:, :width_here].reshape(block_count, BLK, width_here)
    rest = jnp.roll(projected, -head_rank * own_rows, axis=0)[own_rows:]
    k_rest, v_rest = split_kv(rest, width_here, block_count - own_blocks)
    kb, vb = window_of(k_rest), window_of(v_rest)

    keys_t, values = split_kv(projected, width_here, block_count)
    seq_count = lax.axis_size("seq")
    seq_rank = lax.axis_index("seq")
    kanc = gather_all(keys_t[0], "seq")
    vanc = gather_all(values[0], "seq")
    held_count = kanc.shape[0]
    first_block = (seq_rank - 2) * block_count

    rel = jnp.clip(neighbours - first_block, 0, 5 * block_count - 1)
    offset_idx = rel // block_count
    within = rel % block_count
    chunk = within // own_blocks
    inner = within % own_blocks
    mine = chunk == head_rank
    row_a = offset_idx * own_blocks + inner
    row_b = (offset_idx * (block_count - own_blocks)
             + ((chunk - head_rank) % head_count - 1) * own_blocks + inner)
    near_row = jnp.where(mine, row_a, row_b)
    near_src = jnp.where(mine, 0, 1)
    owner = jnp.clip(anchors // block_count, 0, seq_count - 1)
    anch_row = (owner - seq_rank + held_count - 1) % seq_count
    near_used = jnp.arange(neigh)[None, :] < near_count[:, None]
    repeated = jnp.any(
        (anchors[:, :, None] == neighbours[:, None, :]) & near_used[:, None, :], axis=2
    )
    valid = jnp.concatenate([near_used, jnp.logical_not(repeated)], axis=1)
    order = jnp.argsort(jnp.logical_not(valid).astype(jnp.int32), axis=1, stable=True)
    every_row = jnp.concatenate([near_row, anch_row], axis=1)
    every_src = jnp.concatenate([near_src, jnp.full_like(anch_row, 2)], axis=1)
    rows = jnp.take_along_axis(every_row, order, axis=1).astype(jnp.int32)
    source = jnp.take_along_axis(every_src, order, axis=1).astype(jnp.int32)
    count = jnp.sum(valid.astype(jnp.int32), axis=1).astype(jnp.int32)

    attended = attention(queries, (ka, va, kb, vb, kanc, vanc), count, source, rows)
    attended = attended.reshape(row_count, width_here)
    mine_rows = lax.all_to_all(attended, "head", 0, 1, tiled=True)
    mixed_out = jnp.dot(mine_rows, w_out, preferred_element_type=jnp.float32).astype(
        jnp.bfloat16
    )
    return mixed_out


def solution(mesh):
    placed = (P(("seq", "head"), None), P(), P(), P("seq", None), P("seq"), P("seq", None))
    return jax.shard_map(
        shards, mesh=mesh, in_specs=placed, out_specs=P(("seq", "head"), None), check_vma=False
    )
```

```python
import functools

import jax
import jax.numpy as jnp
from jax import lax
from jax.experimental import pallas as pl
from jax.experimental.pallas import tpu as pltpu
from jax.sharding import PartitionSpec as P

D = 768
HDIM = 64
BLK = 128


def shifted(x, axis, by):
    size = lax.axis_size(axis)
    pairs = [(i, i + by) for i in range(size) if 0 <= i + by < size]
    return lax.ppermute(x, axis, pairs)


def gather_all(x, axis):
    size = lax.axis_size(axis)
    rank = lax.axis_index(axis)
    held = x[None]
    step = 1
    while step < size:
        pairs = [(i, (i + step) % size) for i in range(size)]
        got = lax.ppermute(held, axis, pairs)
        held = jnp.concatenate([got, held], axis=0)
        step *= 2
    return held


def attention_kernel(count, source, rows, q_ref, *refs, heads, widths, scale):
    tables = refs[:6]
    o_ref, kt_ref, v_ref = refs[6:]
    b = pl.program_id(0)
    used = count[b]

    @pl.when(b == 0)
    def _():
        kt_ref[...] = jnp.zeros_like(kt_ref)
        v_ref[...] = jnp.zeros_like(v_ref)

    def fetch(j, carry):
        at = pl.multiple_of(j * BLK, BLK)
        row = rows[b, j]
        for code in range(3):
            @pl.when(source[b, j] == code)
            def _():
                kt_ref[:, pl.ds(at, BLK)] = tables[2 * code][row]
                v_ref[pl.ds(at, BLK), :] = tables[2 * code + 1][row]

        return carry

    lax.fori_loop(0, used, fetch, 0)
    limit = used * BLK

    def run(slots):
        span = slots * BLK
        lane = lax.broadcasted_iota(jnp.int32, (1, span), 1)
        bias = jnp.where(lane < limit, 0.0, -jnp.inf)
        for h in range(heads):
            cols = slice(h * HDIM, (h + 1) * HDIM)
            qh = (q_ref[0, :, cols].astype(jnp.float32) * scale).astype(jnp.bfloat16)
            s = jnp.dot(qh, kt_ref[cols, 0:span], preferred_element_type=jnp.float32) + bias
            peak = jnp.max(s, axis=-1, keepdims=True)
            e = jnp.exp(s - peak)
            totals = jnp.sum(e, axis=-1, keepdims=True)
            summed = jnp.dot(e.astype(jnp.bfloat16), v_ref[0:span, cols],
                             preferred_element_type=jnp.float32)
            o_ref[0, :, cols] = (summed / totals).astype(o_ref.dtype)

    low = 0
    for slots in widths:
        @pl.when((used > low) & (used <= slots))
        def _():
            run(slots)
        low = slots


def attention(queries, tables, count, source, rows, widths=None):
    block_count, _, width = queries.shape
    heads = width // HDIM
    slots = rows.shape[1]
    if widths is None:
        widths = tuple(w for w in (8, 12, 16) if w < slots) + (slots,)
    kernel = functools.partial(attention_kernel, heads=heads, widths=widths,
                               scale=HDIM ** (-0.5))
    whole = pl.BlockSpec(memory_space=pltpu.VMEM)
    keys = slots * BLK
    return pl.pallas_call(
        kernel,
        out_shape=jax.ShapeDtypeStruct(queries.shape, jnp.bfloat16),
        grid_spec=pltpu.PrefetchScalarGridSpec(
            num_scalar_prefetch=3,
            grid=(block_count,),
            in_specs=[
                pl.BlockSpec((1, BLK, width), lambda b, *_: (b, 0, 0)),
            ] + [whole] * len(tables),
            out_specs=pl.BlockSpec((1, BLK, width), lambda b, *_: (b, 0, 0)),
            scratch_shapes=[
                pltpu.VMEM((width, keys), jnp.bfloat16),
                pltpu.VMEM((keys, width), jnp.bfloat16),
            ],
        ),
        compiler_params=pltpu.CompilerParams(vmem_limit_bytes=60 * 1024 * 1024),
    )(count, source, rows, queries, *tables)


def split_kv(projected, width, block_count):
    keys_t = jnp.transpose(
        projected[:, width:2 * width].reshape(block_count, BLK, width), (0, 2, 1)
    )
    values = projected[:, 2 * width:].reshape(block_count, BLK, width)
    return keys_t, values


def window_of(x):
    parts = []
    for offset in (2, 1, 0, -1, -2):
        parts.append(x if offset == 0 else shifted(x, "seq", offset))
    return jnp.concatenate(parts, axis=0)


def shards(tokens, w_qkv, w_out, neighbours, near_count, anchors):
    head_count = lax.axis_size("head")
    head_rank = lax.axis_index("head")
    width_here = D // head_count
    own_rows = tokens.shape[0]
    own_blocks = own_rows // BLK
    row_count = own_rows * head_count
    block_count = row_count // BLK
    neigh = neighbours.shape[1]
    col_start = head_rank * width_here
    query_cols = lax.dynamic_slice_in_dim(w_qkv[:, 0], col_start, width_here, 1)
    key_cols = lax.dynamic_slice_in_dim(w_qkv[:, 1], col_start, width_here, 1)
    value_cols = lax.dynamic_slice_in_dim(w_qkv[:, 2], col_start, width_here, 1)
    own_weights = jnp.concatenate([query_cols, key_cols, value_cols], axis=1)

    own_proj = jnp.dot(tokens, own_weights, preferred_element_type=jnp.float32).astype(
        jnp.bfloat16
    )
    k_own, v_own = split_kv(own_proj, width_here, own_blocks)
    ka, va = window_of(k_own), window_of(v_own)

    gathered = lax.all_gather(tokens, "head", axis=0, tiled=True)
    projected = jnp.dot(gathered, own_weights, preferred_element_type=jnp.float32).astype(
        jnp.bfloat16
    )
    queries = projected[:, :width_here].reshape(block_count, BLK, width_here)
    rest = jnp.roll(projected, -head_rank * own_rows, axis=0)[own_rows:]
    k_rest, v_rest = split_kv(rest, width_here, block_count - own_blocks)
    kb, vb = window_of(k_rest), window_of(v_rest)

    keys_t, values = split_kv(projected, width_here, block_count)
    seq_count = lax.axis_size("seq")
    seq_rank = lax.axis_index("seq")
    kanc = gather_all(keys_t[0], "seq")
    vanc = gather_all(values[0], "seq")
    held_count = kanc.shape[0]
    first_block = (seq_rank - 2) * block_count

    rel = jnp.clip(neighbours - first_block, 0, 5 * block_count - 1)
    offset_idx = rel // block_count
    within = rel % block_count
    chunk = within // own_blocks
    inner = within % own_blocks
    mine = chunk == head_rank
    row_a = offset_idx * own_blocks + inner
    row_b = (offset_idx * (block_count - own_blocks)
             + ((chunk - head_rank) % head_count - 1) * own_blocks + inner)
    near_row = jnp.where(mine, row_a, row_b)
    near_src = jnp.where(mine, 0, 1)
    owner = jnp.clip(anchors // block_count, 0, seq_count - 1)
    anch_row = (owner - seq_rank + held_count - 1) % seq_count
    near_used = jnp.arange(neigh)[None, :] < near_count[:, None]
    repeated = jnp.any(
        (anchors[:, :, None] == neighbours[:, None, :]) & near_used[:, None, :], axis=2
    )
    valid = jnp.concatenate([near_used, jnp.logical_not(repeated)], axis=1)
    order = jnp.argsort(jnp.logical_not(valid).astype(jnp.int32), axis=1, stable=True)
    every_row = jnp.concatenate([near_row, anch_row], axis=1)
    every_src = jnp.concatenate([near_src, jnp.full_like(anch_row, 2)], axis=1)
    rows = jnp.take_along_axis(every_row, order, axis=1).astype(jnp.int32)
    source = jnp.take_along_axis(every_src, order, axis=1).astype(jnp.int32)
    count = jnp.sum(valid.astype(jnp.int32), axis=1).astype(jnp.int32)

    attended = attention(queries, (ka, va, kb, vb, kanc, vanc), count, source, rows)
    attended = attended.reshape(row_count, width_here)
    mine_rows = lax.all_to_all(attended, "head", 0, 1, tiled=True)
    mixed_out = jnp.dot(mine_rows, w_out, preferred_element_type=jnp.float32).astype(
        jnp.bfloat16
    )
    return mixed_out


def solution(mesh):
    placed = (P(("seq", "head"), None), P(), P(), P("seq", None), P("seq"), P("seq", None))
    return jax.shard_map(
        shards, mesh=mesh, in_specs=placed, out_specs=P(("seq", "head"), None), check_vma=False
    )
```

```python
import functools

import jax
import jax.numpy as jnp
from jax import lax
from jax.experimental import pallas as pl
from jax.experimental.pallas import tpu as pltpu
from jax.sharding import PartitionSpec as P

D = 768
HDIM = 64
BLK = 128


def shifted(x, axis, by):
    size = lax.axis_size(axis)
    pairs = [(i, i + by) for i in range(size) if 0 <= i + by < size]
    return lax.ppermute(x, axis, pairs)


def gather_all(x, axis):
    size = lax.axis_size(axis)
    rank = lax.axis_index(axis)
    held = x[None]
    step = 1
    while step < size:
        pairs = [(i, (i + step) % size) for i in range(size)]
        got = lax.ppermute(held, axis, pairs)
        held = jnp.concatenate([got, held], axis=0)
        step *= 2
    return held


def attention_kernel(count, source, rows, q_ref, *refs, heads, widths, scale):
    tables = refs[:6]
    o_ref, kt_ref, v_ref = refs[6:]
    b = pl.program_id(0)
    used = count[b]

    @pl.when(b == 0)
    def _():
        kt_ref[...] = jnp.zeros_like(kt_ref)
        v_ref[...] = jnp.zeros_like(v_ref)

    def fetch(j, carry):
        at = pl.multiple_of(j * BLK, BLK)
        row = rows[b, j]
        for code in range(3):
            @pl.when(source[b, j] == code)
            def _():
                start = pl.multiple_of(row * BLK, BLK)
                kt_ref[:, pl.ds(at, BLK)] = tables[2 * code][:, pl.ds(start, BLK)]
                v_ref[pl.ds(at, BLK), :] = tables[2 * code + 1][pl.ds(start, BLK), :]

        return carry

    lax.fori_loop(0, used, fetch, 0)
    limit = used * BLK

    def run(slots):
        span = slots * BLK
        lane = lax.broadcasted_iota(jnp.int32, (1, span), 1)
        bias = jnp.where(lane < limit, 0.0, -jnp.inf)
        for h in range(heads):
            cols = slice(h * HDIM, (h + 1) * HDIM)
            qh = (q_ref[0, :, cols].astype(jnp.float32) * scale).astype(jnp.bfloat16)
            s = jnp.dot(qh, kt_ref[cols, 0:span], preferred_element_type=jnp.float32) + bias
            peak = jnp.max(s, axis=-1, keepdims=True)
            e = jnp.exp(s - peak)
            totals = jnp.sum(e, axis=-1, keepdims=True)
            summed = jnp.dot(e.astype(jnp.bfloat16), v_ref[0:span, cols],
                             preferred_element_type=jnp.float32)
            o_ref[0, :, cols] = (summed / totals).astype(o_ref.dtype)

    low = 0
    for slots in widths:
        @pl.when((used > low) & (used <= slots))
        def _():
            run(slots)
        low = slots


def attention(queries, tables, count, source, rows, widths=None):
    block_count, _, width = queries.shape
    heads = width // HDIM
    slots = rows.shape[1]
    if widths is None:
        widths = tuple(w for w in (8, 12, 16) if w < slots) + (slots,)
    kernel = functools.partial(attention_kernel, heads=heads, widths=widths,
                               scale=HDIM ** (-0.5))
    whole = pl.BlockSpec(memory_space=pltpu.VMEM)
    keys = slots * BLK
    return pl.pallas_call(
        kernel,
        out_shape=jax.ShapeDtypeStruct(queries.shape, jnp.bfloat16),
        grid_spec=pltpu.PrefetchScalarGridSpec(
            num_scalar_prefetch=3,
            grid=(block_count,),
            in_specs=[
                pl.BlockSpec((1, BLK, width), lambda b, *_: (b, 0, 0)),
            ] + [whole] * len(tables),
            out_specs=pl.BlockSpec((1, BLK, width), lambda b, *_: (b, 0, 0)),
            scratch_shapes=[
                pltpu.VMEM((width, keys), jnp.bfloat16),
                pltpu.VMEM((keys, width), jnp.bfloat16),
            ],
        ),
        compiler_params=pltpu.CompilerParams(vmem_limit_bytes=60 * 1024 * 1024),
    )(count, source, rows, queries, *tables)


def project_kv(x, key_w, value_w):
    keys_t = lax.dot_general(key_w, x, (((0,), (1,)), ((), ())),
                             preferred_element_type=jnp.float32).astype(jnp.bfloat16)
    values = jnp.dot(x, value_w, preferred_element_type=jnp.float32).astype(jnp.bfloat16)
    return keys_t, values


def window_of(x, axis):
    parts = []
    for offset in (2, 1, 0, -1, -2):
        parts.append(x if offset == 0 else shifted(x, "seq", offset))
    return jnp.concatenate(parts, axis=axis)


def shards(tokens, w_qkv, w_out, neighbours, near_count, anchors):
    head_count = lax.axis_size("head")
    head_rank = lax.axis_index("head")
    width_here = D // head_count
    own_rows = tokens.shape[0]
    own_blocks = own_rows // BLK
    row_count = own_rows * head_count
    block_count = row_count // BLK
    neigh = neighbours.shape[1]
    col_start = head_rank * width_here
    query_w = lax.dynamic_slice_in_dim(w_qkv[:, 0], col_start, width_here, 1)
    key_w = lax.dynamic_slice_in_dim(w_qkv[:, 1], col_start, width_here, 1)
    value_w = lax.dynamic_slice_in_dim(w_qkv[:, 2], col_start, width_here, 1)

    k_own, v_own = project_kv(tokens, key_w, value_w)
    ka, va = window_of(k_own, 1), window_of(v_own, 0)

    gathered = lax.all_gather(tokens, "head", axis=0, tiled=True)
    rest_tokens = jnp.roll(gathered, -head_rank * own_rows, axis=0)[own_rows:]
    k_rest, v_rest = project_kv(rest_tokens, key_w, value_w)
    kb, vb = window_of(k_rest, 1), window_of(v_rest, 0)
    rolled_tokens = jnp.concatenate([tokens, rest_tokens], axis=0)
    queries = jnp.dot(rolled_tokens, query_w, preferred_element_type=jnp.float32).astype(
        jnp.bfloat16
    ).reshape(block_count, BLK, width_here)

    seq_count = lax.axis_size("seq")
    seq_rank = lax.axis_index("seq")
    k_first, v_first = project_kv(gathered[:BLK], key_w, value_w)
    kanc = gather_all(k_first, "seq")
    vanc = gather_all(v_first, "seq")
    held_count = kanc.shape[0]
    kanc = jnp.transpose(kanc, (1, 0, 2)).reshape(width_here, held_count * BLK)
    vanc = vanc.reshape(held_count * BLK, width_here)
    first_block = (seq_rank - 2) * block_count

    shift = -head_rank * own_blocks
    neighbours = jnp.roll(neighbours, shift, axis=0)
    near_count = jnp.roll(near_count, shift, axis=0)
    anchors = jnp.roll(anchors, shift, axis=0)

    rel = jnp.clip(neighbours - first_block, 0, 5 * block_count - 1)
    offset_idx = rel // block_count
    within = rel % block_count
    chunk = within // own_blocks
    inner = within % own_blocks
    mine = chunk == head_rank
    row_a = offset_idx * own_blocks + inner
    row_b = (offset_idx * (block_count - own_blocks)
             + ((chunk - head_rank) % head_count - 1) * own_blocks + inner)
    near_row = jnp.where(mine, row_a, row_b)
    near_src = jnp.where(mine, 0, 1)
    owner = jnp.clip(anchors // block_count, 0, seq_count - 1)
    anch_row = (owner - seq_rank + held_count - 1) % seq_count
    near_used = jnp.arange(neigh)[None, :] < near_count[:, None]
    repeated = jnp.any(
        (anchors[:, :, None] == neighbours[:, None, :]) & near_used[:, None, :], axis=2
    )
    valid = jnp.concatenate([near_used, jnp.logical_not(repeated)], axis=1)
    order = jnp.argsort(jnp.logical_not(valid).astype(jnp.int32), axis=1, stable=True)
    every_row = jnp.concatenate([near_row, anch_row], axis=1)
    every_src = jnp.concatenate([near_src, jnp.full_like(anch_row, 2)], axis=1)
    rows = jnp.take_along_axis(every_row, order, axis=1).astype(jnp.int32)
    source = jnp.take_along_axis(every_src, order, axis=1).astype(jnp.int32)
    count = jnp.sum(valid.astype(jnp.int32), axis=1).astype(jnp.int32)

    attended = attention(queries, (ka, va, kb, vb, kanc, vanc), count, source, rows)
    attended = jnp.roll(attended.reshape(row_count, width_here), head_rank * own_rows, axis=0)
    mine_rows = lax.all_to_all(attended, "head", 0, 1, tiled=True)
    mixed_out = jnp.dot(mine_rows, w_out, preferred_element_type=jnp.float32).astype(
        jnp.bfloat16
    )
    return mixed_out


def solution(mesh):
    placed = (P(("seq", "head"), None), P(), P(), P("seq", None), P("seq"), P("seq", None))
    return jax.shard_map(
        shards, mesh=mesh, in_specs=placed, out_specs=P(("seq", "head"), None), check_vma=False
    )
```

```python
import functools

import jax
import jax.numpy as jnp
from jax import lax
from jax.experimental import pallas as pl
from jax.experimental.pallas import tpu as pltpu
from jax.sharding import PartitionSpec as P

D = 768
HDIM = 64
BLK = 128


def shifted(x, axis, by):
    size = lax.axis_size(axis)
    pairs = [(i, i + by) for i in range(size) if 0 <= i + by < size]
    return lax.ppermute(x, axis, pairs)


def gather_all(x, axis):
    size = lax.axis_size(axis)
    rank = lax.axis_index(axis)
    held = x[None]
    step = 1
    while step < size:
        pairs = [(i, (i + step) % size) for i in range(size)]
        got = lax.ppermute(held, axis, pairs)
        held = jnp.concatenate([got, held], axis=0)
        step *= 2
    return held


def attention_kernel(count, source, rows, q_ref, *refs, heads, widths, scale):
    tables = refs[:-3]
    o_ref, kt_ref, v_ref = refs[-3:]
    b = pl.program_id(0)
    used = count[b]

    @pl.when(b == 0)
    def _():
        kt_ref[...] = jnp.zeros_like(kt_ref)
        v_ref[...] = jnp.zeros_like(v_ref)

    def fetch(j, carry):
        at = pl.multiple_of(j * BLK, BLK)
        row = rows[b, j]
        for code in range(len(tables) // 2):
            @pl.when(source[b, j] == code)
            def _():
                start = pl.multiple_of(row * BLK, BLK)
                kt_ref[:, pl.ds(at, BLK)] = tables[2 * code][:, pl.ds(start, BLK)]
                v_ref[pl.ds(at, BLK), :] = tables[2 * code + 1][pl.ds(start, BLK), :]

        return carry

    lax.fori_loop(0, used, fetch, 0)
    limit = used * BLK

    def run(slots):
        span = slots * BLK
        lane = lax.broadcasted_iota(jnp.int32, (1, span), 1)
        bias = jnp.where(lane < limit, 0.0, -jnp.inf)
        for h in range(heads):
            cols = slice(h * HDIM, (h + 1) * HDIM)
            qh = (q_ref[0, :, cols].astype(jnp.float32) * scale).astype(jnp.bfloat16)
            s = jnp.dot(qh, kt_ref[cols, 0:span], preferred_element_type=jnp.float32) + bias
            peak = jnp.max(s, axis=-1, keepdims=True)
            e = jnp.exp(s - peak)
            totals = jnp.sum(e, axis=-1, keepdims=True)
            summed = jnp.dot(e.astype(jnp.bfloat16), v_ref[0:span, cols],
                             preferred_element_type=jnp.float32)
            o_ref[0, :, cols] = (summed / totals).astype(o_ref.dtype)

    low = 0
    for slots in widths:
        @pl.when((used > low) & (used <= slots))
        def _():
            run(slots)
        low = slots


def attention(queries, tables, count, source, rows, widths=None):
    block_count, _, width = queries.shape
    heads = width // HDIM
    slots = rows.shape[1]
    if widths is None:
        widths = tuple(w for w in (8, 12, 16) if w < slots) + (slots,)
    kernel = functools.partial(attention_kernel, heads=heads, widths=widths,
                               scale=HDIM ** (-0.5))
    whole = pl.BlockSpec(memory_space=pltpu.VMEM)
    keys = slots * BLK
    return pl.pallas_call(
        kernel,
        out_shape=jax.ShapeDtypeStruct(queries.shape, jnp.bfloat16),
        grid_spec=pltpu.PrefetchScalarGridSpec(
            num_scalar_prefetch=3,
            grid=(block_count,),
            in_specs=[
                pl.BlockSpec((1, BLK, width), lambda b, *_: (b, 0, 0)),
            ] + [whole] * len(tables),
            out_specs=pl.BlockSpec((1, BLK, width), lambda b, *_: (b, 0, 0)),
            scratch_shapes=[
                pltpu.VMEM((width, keys), jnp.bfloat16),
                pltpu.VMEM((keys, width), jnp.bfloat16),
            ],
        ),
        compiler_params=pltpu.CompilerParams(vmem_limit_bytes=60 * 1024 * 1024),
    )(count, source, rows, queries, *tables)


def project_kv(x, key_w, value_w):
    keys_t = lax.dot_general(key_w, x, (((0,), (1,)), ((), ())),
                             preferred_element_type=jnp.float32).astype(jnp.bfloat16)
    values = jnp.dot(x, value_w, preferred_element_type=jnp.float32).astype(jnp.bfloat16)
    return keys_t, values


def window_of(x, axis):
    parts = []
    for offset in (2, 1, 0, -1, -2):
        parts.append(x if offset == 0 else shifted(x, "seq", offset))
    return jnp.concatenate(parts, axis=axis)


def shards(tokens, w_qkv, w_out, neighbours, near_count, anchors):
    head_count = lax.axis_size("head")
    head_rank = lax.axis_index("head")
    width_here = D // head_count
    own_rows = tokens.shape[0]
    own_blocks = own_rows // BLK
    parts = 2 if own_blocks % 2 == 0 else 1
    part_rows = own_rows // parts
    part_blocks = own_blocks // parts
    row_count = own_rows * head_count
    block_count = row_count // BLK
    neigh = neighbours.shape[1]
    col_start = head_rank * width_here
    query_w = lax.dynamic_slice_in_dim(w_qkv[:, 0], col_start, width_here, 1)
    key_w = lax.dynamic_slice_in_dim(w_qkv[:, 1], col_start, width_here, 1)
    value_w = lax.dynamic_slice_in_dim(w_qkv[:, 2], col_start, width_here, 1)

    k_own, v_own = project_kv(tokens, key_w, value_w)
    tables = [window_of(k_own, 1), window_of(v_own, 0)]

    rest_parts = []
    first_rows = None
    for p in range(parts):
        piece = tokens[p * part_rows:(p + 1) * part_rows]
        gathered = lax.all_gather(piece, "head", axis=0, tiled=True)
        if p == 0:
            first_rows = gathered[:BLK]
        rest = jnp.roll(gathered, -head_rank * part_rows, axis=0)[part_rows:]
        k_rest, v_rest = project_kv(rest, key_w, value_w)
        tables += [window_of(k_rest, 1), window_of(v_rest, 0)]
        rest_parts.append(rest.reshape(head_count - 1, part_rows, D))
    rest_tokens = jnp.concatenate(rest_parts, axis=1).reshape((head_count - 1) * own_rows, D)
    rolled_tokens = jnp.concatenate([tokens, rest_tokens], axis=0)
    queries = jnp.dot(rolled_tokens, query_w, preferred_element_type=jnp.float32).astype(
        jnp.bfloat16
    ).reshape(block_count, BLK, width_here)

    seq_count = lax.axis_size("seq")
    seq_rank = lax.axis_index("seq")
    k_first, v_first = project_kv(first_rows, key_w, value_w)
    kanc = gather_all(k_first, "seq")
    vanc = gather_all(v_first, "seq")
    held_count = kanc.shape[0]
    kanc = jnp.transpose(kanc, (1, 0, 2)).reshape(width_here, held_count * BLK)
    vanc = vanc.reshape(held_count * BLK, width_here)
    tables += [kanc, vanc]
    first_block = (seq_rank - 2) * block_count

    shift = -head_rank * own_blocks
    neighbours = jnp.roll(neighbours, shift, axis=0)
    near_count = jnp.roll(near_count, shift, axis=0)
    anchors = jnp.roll(anchors, shift, axis=0)

    rel = jnp.clip(neighbours - first_block, 0, 5 * block_count - 1)
    offset_idx = rel // block_count
    within = rel % block_count
    chunk = within // own_blocks
    inner = within % own_blocks
    mine = chunk == head_rank
    row_a = offset_idx * own_blocks + inner
    row_b = (offset_idx * (head_count - 1) * part_blocks
             + ((chunk - head_rank) % head_count - 1) * part_blocks + inner % part_blocks)
    near_row = jnp.where(mine, row_a, row_b)
    near_src = jnp.where(mine, 0, 1 + inner // part_blocks)
    owner = jnp.clip(anchors // block_count, 0, seq_count - 1)
    anch_row = (owner - seq_rank + held_count - 1) % seq_count
    near_used = jnp.arange(neigh)[None, :] < near_count[:, None]
    repeated = jnp.any(
        (anchors[:, :, None] == neighbours[:, None, :]) & near_used[:, None, :], axis=2
    )
    valid = jnp.concatenate([near_used, jnp.logical_not(repeated)], axis=1)
    order = jnp.argsort(jnp.logical_not(valid).astype(jnp.int32), axis=1, stable=True)
    every_row = jnp.concatenate([near_row, anch_row], axis=1)
    every_src = jnp.concatenate([near_src, jnp.full_like(anch_row, 1 + parts)], axis=1)
    rows = jnp.take_along_axis(every_row, order, axis=1).astype(jnp.int32)
    source = jnp.take_along_axis(every_src, order, axis=1).astype(jnp.int32)
    count = jnp.sum(valid.astype(jnp.int32), axis=1).astype(jnp.int32)

    attended = attention(queries, tuple(tables), count, source, rows)
    attended = jnp.roll(attended.reshape(row_count, width_here), head_rank * own_rows, axis=0)
    mine_rows = lax.all_to_all(attended, "head", 0, 1, tiled=True)
    mixed_out = jnp.dot(mine_rows, w_out, preferred_element_type=jnp.float32).astype(
        jnp.bfloat16
    )
    return mixed_out


def solution(mesh):
    placed = (P(("seq", "head"), None), P(), P(), P("seq", None), P("seq"), P("seq", None))
    return jax.shard_map(
        shards, mesh=mesh, in_specs=placed, out_specs=P(("seq", "head"), None), check_vma=False
    )
```

```python
import functools

import jax
import jax.numpy as jnp
from jax import lax
from jax.experimental import pallas as pl
from jax.experimental.pallas import tpu as pltpu
from jax.sharding import PartitionSpec as P

D = 768
HDIM = 64
BLK = 128


def shifted(x, axis, by):
    size = lax.axis_size(axis)
    pairs = [(i, i + by) for i in range(size) if 0 <= i + by < size]
    return lax.ppermute(x, axis, pairs)


def gather_all(x, axis):
    size = lax.axis_size(axis)
    rank = lax.axis_index(axis)
    held = x[None]
    step = 1
    while step < size:
        pairs = [(i, (i + step) % size) for i in range(size)]
        got = lax.ppermute(held, axis, pairs)
        held = jnp.concatenate([got, held], axis=0)
        step *= 2
    return held


def attention_kernel(count, source, rows, q_ref, *refs, heads, widths, scale):
    tables = refs[:-2]
    o_ref, kv_ref = refs[-2:]
    b = pl.program_id(0)
    used = count[b]

    @pl.when(b == 0)
    def _():
        kv_ref[...] = jnp.zeros_like(kv_ref)

    def fetch(j, carry):
        at = pl.multiple_of(j * BLK, BLK)
        row = rows[b, j]
        for code in range(len(tables)):
            @pl.when(source[b, j] == code)
            def _():
                start = pl.multiple_of(row * BLK, BLK)
                kv_ref[pl.ds(at, BLK), :] = tables[code][pl.ds(start, BLK), :]

        return carry

    lax.fori_loop(0, used, fetch, 0)
    limit = used * BLK

    width = heads * HDIM

    def run(slots):
        span = slots * BLK
        lane = lax.broadcasted_iota(jnp.int32, (1, span), 1)
        bias = jnp.where(lane < limit, 0.0, -jnp.inf)
        for h in range(heads):
            cols = slice(h * HDIM, (h + 1) * HDIM)
            qh = (q_ref[0, :, cols].astype(jnp.float32) * scale).astype(jnp.bfloat16)
            s = lax.dot_general(qh, kv_ref[0:span, cols], (((1,), (1,)), ((), ())),
                                preferred_element_type=jnp.float32) + bias
            peak = jnp.max(s, axis=-1, keepdims=True)
            e = jnp.exp(s - peak)
            totals = jnp.sum(e, axis=-1, keepdims=True)
            vcols = slice(width + h * HDIM, width + (h + 1) * HDIM)
            summed = jnp.dot(e.astype(jnp.bfloat16), kv_ref[0:span, vcols],
                             preferred_element_type=jnp.float32)
            o_ref[0, :, cols] = (summed / totals).astype(o_ref.dtype)

    low = 0
    for slots in widths:
        @pl.when((used > low) & (used <= slots))
        def _():
            run(slots)
        low = slots


def attention(queries, tables, count, source, rows, widths=None):
    block_count, _, width = queries.shape
    heads = width // HDIM
    slots = rows.shape[1]
    if widths is None:
        widths = tuple(w for w in (8, 12, 16) if w < slots) + (slots,)
    kernel = functools.partial(attention_kernel, heads=heads, widths=widths,
                               scale=HDIM ** (-0.5))
    whole = pl.BlockSpec(memory_space=pltpu.VMEM)
    keys = slots * BLK
    return pl.pallas_call(
        kernel,
        out_shape=jax.ShapeDtypeStruct(queries.shape, jnp.bfloat16),
        grid_spec=pltpu.PrefetchScalarGridSpec(
            num_scalar_prefetch=3,
            grid=(block_count,),
            in_specs=[
                pl.BlockSpec((1, BLK, width), lambda b, *_: (b, 0, 0)),
            ] + [whole] * len(tables),
            out_specs=pl.BlockSpec((1, BLK, width), lambda b, *_: (b, 0, 0)),
            scratch_shapes=[
                pltpu.VMEM((keys, 2 * width), jnp.bfloat16),
            ],
        ),
        compiler_params=pltpu.CompilerParams(vmem_limit_bytes=60 * 1024 * 1024),
    )(count, source, rows, queries, *tables)


def project_kv(x, kv_w):
    return jnp.dot(x, kv_w, preferred_element_type=jnp.float32).astype(jnp.bfloat16)


def window_of(x, axis):
    parts = []
    for offset in (2, 1, 0, -1, -2):
        parts.append(x if offset == 0 else shifted(x, "seq", offset))
    return jnp.concatenate(parts, axis=axis)


def shards(tokens, w_qkv, w_out, neighbours, near_count, anchors):
    head_count = lax.axis_size("head")
    head_rank = lax.axis_index("head")
    width_here = D // head_count
    own_rows = tokens.shape[0]
    own_blocks = own_rows // BLK
    row_count = own_rows * head_count
    block_count = row_count // BLK
    neigh = neighbours.shape[1]
    col_start = head_rank * width_here
    query_w = lax.dynamic_slice_in_dim(w_qkv[:, 0], col_start, width_here, 1)
    key_w = lax.dynamic_slice_in_dim(w_qkv[:, 1], col_start, width_here, 1)
    value_w = lax.dynamic_slice_in_dim(w_qkv[:, 2], col_start, width_here, 1)

    kv_w = jnp.concatenate([key_w, value_w], axis=1)
    kva = window_of(project_kv(tokens, kv_w), 0)

    gathered = lax.all_gather(tokens, "head", axis=0, tiled=True)
    rest_tokens = jnp.roll(gathered, -head_rank * own_rows, axis=0)[own_rows:]
    kvb = window_of(project_kv(rest_tokens, kv_w), 0)
    rolled_tokens = jnp.concatenate([tokens, rest_tokens], axis=0)
    queries = jnp.dot(rolled_tokens, query_w, preferred_element_type=jnp.float32).astype(
        jnp.bfloat16
    ).reshape(block_count, BLK, width_here)

    seq_count = lax.axis_size("seq")
    seq_rank = lax.axis_index("seq")
    kvanc = gather_all(project_kv(gathered[:BLK], kv_w), "seq")
    held_count = kvanc.shape[0]
    kvanc = kvanc.reshape(held_count * BLK, 2 * width_here)
    first_block = (seq_rank - 2) * block_count

    shift = -head_rank * own_blocks
    neighbours = jnp.roll(neighbours, shift, axis=0)
    near_count = jnp.roll(near_count, shift, axis=0)
    anchors = jnp.roll(anchors, shift, axis=0)

    rel = jnp.clip(neighbours - first_block, 0, 5 * block_count - 1)
    offset_idx = rel // block_count
    within = rel % block_count
    chunk = within // own_blocks
    inner = within % own_blocks
    mine = chunk == head_rank
    row_a = offset_idx * own_blocks + inner
    row_b = (offset_idx * (block_count - own_blocks)
             + ((chunk - head_rank) % head_count - 1) * own_blocks + inner)
    near_row = jnp.where(mine, row_a, row_b)
    near_src = jnp.where(mine, 0, 1)
    owner = jnp.clip(anchors // block_count, 0, seq_count - 1)
    anch_row = (owner - seq_rank + held_count - 1) % seq_count
    near_used = jnp.arange(neigh)[None, :] < near_count[:, None]
    repeated = jnp.any(
        (anchors[:, :, None] == neighbours[:, None, :]) & near_used[:, None, :], axis=2
    )
    valid = jnp.concatenate([near_used, jnp.logical_not(repeated)], axis=1)
    order = jnp.argsort(jnp.logical_not(valid).astype(jnp.int32), axis=1, stable=True)
    every_row = jnp.concatenate([near_row, anch_row], axis=1)
    every_src = jnp.concatenate([near_src, jnp.full_like(anch_row, 2)], axis=1)
    rows = jnp.take_along_axis(every_row, order, axis=1).astype(jnp.int32)
    source = jnp.take_along_axis(every_src, order, axis=1).astype(jnp.int32)
    count = jnp.sum(valid.astype(jnp.int32), axis=1).astype(jnp.int32)

    attended = attention(queries, (kva, kvb, kvanc), count, source, rows)
    attended = jnp.roll(attended.reshape(row_count, width_here), head_rank * own_rows, axis=0)
    mine_rows = lax.all_to_all(attended, "head", 0, 1, tiled=True)
    mixed_out = jnp.dot(mine_rows, w_out, preferred_element_type=jnp.float32).astype(
        jnp.bfloat16
    )
    return mixed_out


def solution(mesh):
    placed = (P(("seq", "head"), None), P(), P(), P("seq", None), P("seq"), P("seq", None))
    return jax.shard_map(
        shards, mesh=mesh, in_specs=placed, out_specs=P(("seq", "head"), None), check_vma=False
    )
```

```python
import functools

import jax
import jax.numpy as jnp
from jax import lax
from jax.experimental import pallas as pl
from jax.experimental.pallas import tpu as pltpu
from jax.sharding import PartitionSpec as P

D = 768
HDIM = 64
BLK = 128


def shifted(x, axis, by):
    size = lax.axis_size(axis)
    pairs = [(i, i + by) for i in range(size) if 0 <= i + by < size]
    return lax.ppermute(x, axis, pairs)


def gather_all(x, axis):
    size = lax.axis_size(axis)
    rank = lax.axis_index(axis)
    held = x[None]
    step = 1
    while step < size:
        pairs = [(i, (i + step) % size) for i in range(size)]
        got = lax.ppermute(held, axis, pairs)
        held = jnp.concatenate([got, held], axis=0)
        step *= 2
    return held


def attention_kernel(count, source, rows, q_ref, *refs, heads, widths, scale):
    tables = refs[:-2]
    o_ref, kv_ref = refs[-2:]
    b = pl.program_id(0)
    used = count[b]

    @pl.when(b == 0)
    def _():
        kv_ref[...] = jnp.zeros_like(kv_ref)

    def fetch(j, carry):
        at = pl.multiple_of(j * BLK, BLK)
        row = rows[b, j]
        for code in range(len(tables)):
            @pl.when(source[b, j] == code)
            def _():
                start = pl.multiple_of(row * BLK, BLK)
                kv_ref[pl.ds(at, BLK), :] = tables[code][pl.ds(start, BLK), :]

        return carry

    lax.fori_loop(0, used, fetch, 0)
    limit = used * BLK

    width = heads * HDIM

    def run(slots):
        span = slots * BLK
        lane = lax.broadcasted_iota(jnp.int32, (1, span), 1)
        bias = jnp.where(lane < limit, 0.0, -jnp.inf)
        for h in range(heads):
            cols = slice(h * HDIM, (h + 1) * HDIM)
            qh = (q_ref[0, :, cols].astype(jnp.float32) * scale).astype(jnp.bfloat16)
            s = lax.dot_general(qh, kv_ref[0:span, cols], (((1,), (1,)), ((), ())),
                                preferred_element_type=jnp.float32) + bias
            peak = jnp.max(s, axis=-1, keepdims=True)
            e = jnp.exp(s - peak)
            totals = jnp.sum(e, axis=-1, keepdims=True)
            vcols = slice(width + h * HDIM, width + (h + 1) * HDIM)
            summed = jnp.dot(e.astype(jnp.bfloat16), kv_ref[0:span, vcols],
                             preferred_element_type=jnp.float32)
            o_ref[0, :, cols] = (summed / totals).astype(o_ref.dtype)

    low = 0
    for slots in widths:
        @pl.when((used > low) & (used <= slots))
        def _():
            run(slots)
        low = slots


def attention(queries, tables, count, source, rows, widths=None):
    block_count, _, width = queries.shape
    heads = width // HDIM
    slots = rows.shape[1]
    if widths is None:
        widths = tuple(w for w in (8, 12, 16) if w < slots) + (slots,)
    kernel = functools.partial(attention_kernel, heads=heads, widths=widths,
                               scale=HDIM ** (-0.5))
    whole = pl.BlockSpec(memory_space=pltpu.VMEM)
    keys = slots * BLK
    return pl.pallas_call(
        kernel,
        out_shape=jax.ShapeDtypeStruct(queries.shape, jnp.bfloat16),
        grid_spec=pltpu.PrefetchScalarGridSpec(
            num_scalar_prefetch=3,
            grid=(block_count,),
            in_specs=[
                pl.BlockSpec((1, BLK, width), lambda b, *_: (b, 0, 0)),
            ] + [whole] * len(tables),
            out_specs=pl.BlockSpec((1, BLK, width), lambda b, *_: (b, 0, 0)),
            scratch_shapes=[
                pltpu.VMEM((keys, 2 * width), jnp.bfloat16),
            ],
        ),
        compiler_params=pltpu.CompilerParams(vmem_limit_bytes=60 * 1024 * 1024),
        cost_estimate=pl.CostEstimate(
            flops=4 * block_count * BLK * keys * width,
            transcendentals=block_count * heads * BLK * keys,
            bytes_accessed=sum(t.size * t.dtype.itemsize for t in tables) + 2 * queries.size * 2,
        ),
    )(count, source, rows, queries, *tables)


def project_kv(x, kv_w):
    return jnp.dot(x, kv_w, preferred_element_type=jnp.float32).astype(jnp.bfloat16)


def window_of(x, axis):
    parts = []
    for offset in (2, 1, 0, -1, -2):
        parts.append(x if offset == 0 else shifted(x, "seq", offset))
    return jnp.concatenate(parts, axis=axis)


def shards(tokens, w_qkv, w_out, neighbours, near_count, anchors):
    head_count = lax.axis_size("head")
    head_rank = lax.axis_index("head")
    width_here = D // head_count
    own_rows = tokens.shape[0]
    own_blocks = own_rows // BLK
    row_count = own_rows * head_count
    block_count = row_count // BLK
    neigh = neighbours.shape[1]
    col_start = head_rank * width_here
    query_w = lax.dynamic_slice_in_dim(w_qkv[:, 0], col_start, width_here, 1)
    key_w = lax.dynamic_slice_in_dim(w_qkv[:, 1], col_start, width_here, 1)
    value_w = lax.dynamic_slice_in_dim(w_qkv[:, 2], col_start, width_here, 1)

    kv_w = jnp.concatenate([key_w, value_w], axis=1)
    kva = window_of(project_kv(tokens, kv_w), 0)

    gathered = lax.all_gather(tokens, "head", axis=0, tiled=True)
    rest_tokens = jnp.roll(gathered, -head_rank * own_rows, axis=0)[own_rows:]
    kvb = window_of(project_kv(rest_tokens, kv_w), 0)
    rolled_tokens = jnp.concatenate([tokens, rest_tokens], axis=0)
    queries = jnp.dot(rolled_tokens, query_w, preferred_element_type=jnp.float32).astype(
        jnp.bfloat16
    ).reshape(block_count, BLK, width_here)

    seq_count = lax.axis_size("seq")
    seq_rank = lax.axis_index("seq")
    kvanc = gather_all(project_kv(gathered[:BLK], kv_w), "seq")
    held_count = kvanc.shape[0]
    kvanc = kvanc.reshape(held_count * BLK, 2 * width_here)
    first_block = (seq_rank - 2) * block_count

    shift = -head_rank * own_blocks
    neighbours = jnp.roll(neighbours, shift, axis=0)
    near_count = jnp.roll(near_count, shift, axis=0)
    anchors = jnp.roll(anchors, shift, axis=0)

    rel = jnp.clip(neighbours - first_block, 0, 5 * block_count - 1)
    offset_idx = rel // block_count
    within = rel % block_count
    chunk = within // own_blocks
    inner = within % own_blocks
    mine = chunk == head_rank
    row_a = offset_idx * own_blocks + inner
    row_b = (offset_idx * (block_count - own_blocks)
             + ((chunk - head_rank) % head_count - 1) * own_blocks + inner)
    near_row = jnp.where(mine, row_a, row_b)
    near_src = jnp.where(mine, 0, 1)
    owner = jnp.clip(anchors // block_count, 0, seq_count - 1)
    anch_row = (owner - seq_rank + held_count - 1) % seq_count
    near_used = jnp.arange(neigh)[None, :] < near_count[:, None]
    repeated = jnp.any(
        (anchors[:, :, None] == neighbours[:, None, :]) & near_used[:, None, :], axis=2
    )
    valid = jnp.concatenate([near_used, jnp.logical_not(repeated)], axis=1)
    order = jnp.argsort(jnp.logical_not(valid).astype(jnp.int32), axis=1, stable=True)
    every_row = jnp.concatenate([near_row, anch_row], axis=1)
    every_src = jnp.concatenate([near_src, jnp.full_like(anch_row, 2)], axis=1)
    rows = jnp.take_along_axis(every_row, order, axis=1).astype(jnp.int32)
    source = jnp.take_along_axis(every_src, order, axis=1).astype(jnp.int32)
    count = jnp.sum(valid.astype(jnp.int32), axis=1).astype(jnp.int32)

    tables = (kva, kvb, kvanc)
    away = attention(queries[own_blocks:], tables, count[own_blocks:], source[own_blocks:],
                     rows[own_blocks:])
    away = away.reshape(head_count - 1, own_rows, width_here)
    received = [None] * head_count
    for j in range(1, head_count):
        pairs = [(z, (z + j) % head_count) for z in range(head_count)]
        received[j] = lax.ppermute(away[j - 1], "head", pairs)
    received[0] = attention(queries[:own_blocks], tables, count[:own_blocks],
                            source[:own_blocks], rows[:own_blocks]).reshape(own_rows, width_here)
    mine_rows = jnp.concatenate(received, axis=1)
    groups = (head_rank - jnp.arange(head_count)) % head_count
    out_w = jnp.take(w_out.reshape(head_count, width_here, D), groups, axis=0).reshape(D, D)
    mixed_out = jnp.dot(mine_rows, out_w, preferred_element_type=jnp.float32).astype(
        jnp.bfloat16
    )
    return mixed_out


def solution(mesh):
    placed = (P(("seq", "head"), None), P(), P(), P("seq", None), P("seq"), P("seq", None))
    return jax.shard_map(
        shards, mesh=mesh, in_specs=placed, out_specs=P(("seq", "head"), None), check_vma=False
    )
```

```python
import functools

import jax
import jax.numpy as jnp
from jax import lax
from jax.experimental import pallas as pl
from jax.experimental.pallas import tpu as pltpu
from jax.sharding import PartitionSpec as P

D = 768
HDIM = 64
BLK = 128


def shifted(x, axis, by):
    size = lax.axis_size(axis)
    pairs = [(i, i + by) for i in range(size) if 0 <= i + by < size]
    return lax.ppermute(x, axis, pairs)


def gather_all(x, axis):
    size = lax.axis_size(axis)
    rank = lax.axis_index(axis)
    held = x[None]
    step = 1
    while step < size:
        pairs = [(i, (i + step) % size) for i in range(size)]
        got = lax.ppermute(held, axis, pairs)
        held = jnp.concatenate([got, held], axis=0)
        step *= 2
    return held


def attention_kernel(count, source, rows, q_ref, *refs, heads, widths, scale):
    tables = refs[:-2]
    o_ref, kv_ref = refs[-2:]
    b = pl.program_id(0)
    used = count[b]

    @pl.when(b == 0)
    def _():
        kv_ref[...] = jnp.zeros_like(kv_ref)

    def fetch(j, carry):
        at = pl.multiple_of(j * BLK, BLK)
        row = rows[b, j]
        for code in range(len(tables)):
            @pl.when(source[b, j] == code)
            def _():
                start = pl.multiple_of(row * BLK, BLK)
                kv_ref[pl.ds(at, BLK), :] = tables[code][pl.ds(start, BLK), :]

        return carry

    lax.fori_loop(0, used, fetch, 0)
    limit = used * BLK

    width = heads * HDIM

    def run(slots):
        span = slots * BLK
        lane = lax.broadcasted_iota(jnp.int32, (1, span), 1)
        bias = jnp.where(lane < limit, 0.0, -jnp.inf)
        for h in range(heads):
            cols = slice(h * HDIM, (h + 1) * HDIM)
            qh = (q_ref[0, :, cols].astype(jnp.float32) * scale).astype(jnp.bfloat16)
            s = lax.dot_general(qh, kv_ref[0:span, cols], (((1,), (1,)), ((), ())),
                                preferred_element_type=jnp.float32) + bias
            peak = jnp.max(s, axis=-1, keepdims=True)
            e = jnp.exp(s - peak)
            totals = jnp.sum(e, axis=-1, keepdims=True)
            vcols = slice(width + h * HDIM, width + (h + 1) * HDIM)
            summed = jnp.dot(e.astype(jnp.bfloat16), kv_ref[0:span, vcols],
                             preferred_element_type=jnp.float32)
            o_ref[0, :, cols] = (summed / totals).astype(o_ref.dtype)

    low = 0
    for slots in widths:
        @pl.when((used > low) & (used <= slots))
        def _():
            run(slots)
        low = slots


def attention(queries, tables, count, source, rows, widths=None):
    block_count, _, width = queries.shape
    heads = width // HDIM
    slots = rows.shape[1]
    if widths is None:
        widths = tuple(w for w in (8, 12, 16) if w < slots) + (slots,)
    kernel = functools.partial(attention_kernel, heads=heads, widths=widths,
                               scale=HDIM ** (-0.5))
    whole = pl.BlockSpec(memory_space=pltpu.VMEM)
    keys = slots * BLK
    return pl.pallas_call(
        kernel,
        out_shape=jax.ShapeDtypeStruct(queries.shape, jnp.bfloat16),
        grid_spec=pltpu.PrefetchScalarGridSpec(
            num_scalar_prefetch=3,
            grid=(block_count,),
            in_specs=[
                pl.BlockSpec((1, BLK, width), lambda b, *_: (b, 0, 0)),
            ] + [whole] * len(tables),
            out_specs=pl.BlockSpec((1, BLK, width), lambda b, *_: (b, 0, 0)),
            scratch_shapes=[
                pltpu.VMEM((keys, 2 * width), jnp.bfloat16),
            ],
        ),
        compiler_params=pltpu.CompilerParams(vmem_limit_bytes=60 * 1024 * 1024),
        cost_estimate=pl.CostEstimate(
            flops=4 * block_count * BLK * keys * width,
            transcendentals=block_count * heads * BLK * keys,
            bytes_accessed=sum(t.size * t.dtype.itemsize for t in tables) + 2 * queries.size * 2,
        ),
    )(count, source, rows, queries, *tables)


def project_kv(x, kv_w):
    return jnp.dot(x, kv_w, preferred_element_type=jnp.float32).astype(jnp.bfloat16)


def window_of(x, axis):
    size = lax.axis_size("seq")
    beside = {}
    if size == 8:
        plus2 = lax.ppermute(x, "seq", [(i, i + 2) for i in range(6) if i not in (2, 3)])
        minus2 = lax.ppermute(x, "seq", [(i, i - 2) for i in range(2, 8) if i not in (4, 5)])
        beside[2] = plus2 + lax.ppermute(minus2, "seq", [(0, 4), (1, 5)])
        beside[-2] = minus2 + lax.ppermute(plus2, "seq", [(6, 2), (7, 3)])
    else:
        beside[2] = shifted(x, "seq", 2)
        beside[-2] = shifted(x, "seq", -2)
    beside[1] = shifted(x, "seq", 1)
    beside[-1] = shifted(x, "seq", -1)
    beside[0] = x
    return jnp.concatenate([beside[k] for k in (2, 1, 0, -1, -2)], axis=axis)


def shards(tokens, w_qkv, w_out, neighbours, near_count, anchors):
    head_count = lax.axis_size("head")
    head_rank = lax.axis_index("head")
    width_here = D // head_count
    own_rows = tokens.shape[0]
    own_blocks = own_rows // BLK
    row_count = own_rows * head_count
    block_count = row_count // BLK
    neigh = neighbours.shape[1]
    col_start = head_rank * width_here
    query_w = lax.dynamic_slice_in_dim(w_qkv[:, 0], col_start, width_here, 1)
    key_w = lax.dynamic_slice_in_dim(w_qkv[:, 1], col_start, width_here, 1)
    value_w = lax.dynamic_slice_in_dim(w_qkv[:, 2], col_start, width_here, 1)

    kv_w = jnp.concatenate([key_w, value_w], axis=1)
    kva = window_of(project_kv(tokens, kv_w), 0)

    gathered = lax.all_gather(tokens, "head", axis=0, tiled=True)
    rest_tokens = jnp.roll(gathered, -head_rank * own_rows, axis=0)[own_rows:]
    kvb = window_of(project_kv(rest_tokens, kv_w), 0)
    rolled_tokens = jnp.concatenate([tokens, rest_tokens], axis=0)
    queries = jnp.dot(rolled_tokens, query_w, preferred_element_type=jnp.float32).astype(
        jnp.bfloat16
    ).reshape(block_count, BLK, width_here)

    seq_count = lax.axis_size("seq")
    seq_rank = lax.axis_index("seq")
    kvanc = gather_all(project_kv(gathered[:BLK], kv_w), "seq")
    held_count = kvanc.shape[0]
    kvanc = kvanc.reshape(held_count * BLK, 2 * width_here)
    first_block = (seq_rank - 2) * block_count

    shift = -head_rank * own_blocks
    neighbours = jnp.roll(neighbours, shift, axis=0)
    near_count = jnp.roll(near_count, shift, axis=0)
    anchors = jnp.roll(anchors, shift, axis=0)

    rel = jnp.clip(neighbours - first_block, 0, 5 * block_count - 1)
    offset_idx = rel // block_count
    within = rel % block_count
    chunk = within // own_blocks
    inner = within % own_blocks
    mine = chunk == head_rank
    row_a = offset_idx * own_blocks + inner
    row_b = (offset_idx * (block_count - own_blocks)
             + ((chunk - head_rank) % head_count - 1) * own_blocks + inner)
    near_row = jnp.where(mine, row_a, row_b)
    near_src = jnp.where(mine, 0, 1)
    owner = jnp.clip(anchors // block_count, 0, seq_count - 1)
    anch_row = (owner - seq_rank + held_count - 1) % seq_count
    near_used = jnp.arange(neigh)[None, :] < near_count[:, None]
    repeated = jnp.any(
        (anchors[:, :, None] == neighbours[:, None, :]) & near_used[:, None, :], axis=2
    )
    valid = jnp.concatenate([near_used, jnp.logical_not(repeated)], axis=1)
    order = jnp.argsort(jnp.logical_not(valid).astype(jnp.int32), axis=1, stable=True)
    every_row = jnp.concatenate([near_row, anch_row], axis=1)
    every_src = jnp.concatenate([near_src, jnp.full_like(anch_row, 2)], axis=1)
    rows = jnp.take_along_axis(every_row, order, axis=1).astype(jnp.int32)
    source = jnp.take_along_axis(every_src, order, axis=1).astype(jnp.int32)
    count = jnp.sum(valid.astype(jnp.int32), axis=1).astype(jnp.int32)

    tables = (kva, kvb, kvanc)
    away = attention(queries[own_blocks:], tables, count[own_blocks:], source[own_blocks:],
                     rows[own_blocks:])
    away = away.reshape(head_count - 1, own_rows, width_here)
    received = [None] * head_count
    for j in range(1, head_count):
        pairs = [(z, (z + j) % head_count) for z in range(head_count)]
        received[j] = lax.ppermute(away[j - 1], "head", pairs)
    received[0] = attention(queries[:own_blocks], tables, count[:own_blocks],
                            source[:own_blocks], rows[:own_blocks]).reshape(own_rows, width_here)
    mine_rows = jnp.concatenate(received, axis=1)
    groups = (head_rank - jnp.arange(head_count)) % head_count
    out_w = jnp.take(w_out.reshape(head_count, width_here, D), groups, axis=0).reshape(D, D)
    mixed_out = jnp.dot(mine_rows, out_w, preferred_element_type=jnp.float32).astype(
        jnp.bfloat16
    )
    return mixed_out


def solution(mesh):
    placed = (P(("seq", "head"), None), P(), P(), P("seq", None), P("seq"), P("seq", None))
    return jax.shard_map(
        shards, mesh=mesh, in_specs=placed, out_specs=P(("seq", "head"), None), check_vma=False
    )
```

```python
import functools

import jax
import jax.numpy as jnp
from jax import lax
from jax.experimental import pallas as pl
from jax.experimental.pallas import tpu as pltpu
from jax.sharding import PartitionSpec as P

D = 768
HDIM = 64
BLK = 128


def shifted(x, axis, by):
    size = lax.axis_size(axis)
    pairs = [(i, i + by) for i in range(size) if 0 <= i + by < size]
    return lax.ppermute(x, axis, pairs)


def gather_all(x, axis):
    size = lax.axis_size(axis)
    rank = lax.axis_index(axis)
    held = x[None]
    step = 1
    while step < size:
        pairs = [(i, (i + step) % size) for i in range(size)]
        got = lax.ppermute(held, axis, pairs)
        held = jnp.concatenate([got, held], axis=0)
        step *= 2
    return held


def attention_kernel(count, source, rows, q_ref, *refs, heads, widths, scale):
    tables = refs[:-2]
    o_ref, kv_ref = refs[-2:]
    b = pl.program_id(0)
    used = count[b]

    @pl.when(b == 0)
    def _():
        kv_ref[...] = jnp.zeros_like(kv_ref)

    def fetch(j, carry):
        at = pl.multiple_of(j * BLK, BLK)
        row = rows[b, j]
        for code in range(len(tables)):
            @pl.when(source[b, j] == code)
            def _():
                start = pl.multiple_of(row * BLK, BLK)
                kv_ref[pl.ds(at, BLK), :] = tables[code][pl.ds(start, BLK), :]

        return carry

    lax.fori_loop(0, used, fetch, 0)
    limit = used * BLK

    width = heads * HDIM

    def run(slots):
        span = slots * BLK
        lane = lax.broadcasted_iota(jnp.int32, (1, span), 1)
        bias = jnp.where(lane < limit, 0.0, -jnp.inf)
        for h in range(heads):
            cols = slice(h * HDIM, (h + 1) * HDIM)
            qh = (q_ref[0, :, cols].astype(jnp.float32) * scale).astype(jnp.bfloat16)
            s = lax.dot_general(qh, kv_ref[0:span, cols], (((1,), (1,)), ((), ())),
                                preferred_element_type=jnp.float32) + bias
            peak = jnp.max(s, axis=-1, keepdims=True)
            e = jnp.exp(s - peak)
            totals = jnp.sum(e, axis=-1, keepdims=True)
            vcols = slice(width + h * HDIM, width + (h + 1) * HDIM)
            summed = jnp.dot(e.astype(jnp.bfloat16), kv_ref[0:span, vcols],
                             preferred_element_type=jnp.float32)
            o_ref[0, :, cols] = (summed / totals).astype(o_ref.dtype)

    low = 0
    for slots in widths:
        @pl.when((used > low) & (used <= slots))
        def _():
            run(slots)
        low = slots


def attention(queries, tables, count, source, rows, widths=None):
    block_count, _, width = queries.shape
    heads = width // HDIM
    slots = rows.shape[1]
    if widths is None:
        widths = tuple(w for w in (8, 12, 16) if w < slots) + (slots,)
    kernel = functools.partial(attention_kernel, heads=heads, widths=widths,
                               scale=HDIM ** (-0.5))
    whole = pl.BlockSpec(memory_space=pltpu.VMEM)
    keys = slots * BLK
    return pl.pallas_call(
        kernel,
        out_shape=jax.ShapeDtypeStruct(queries.shape, jnp.bfloat16),
        grid_spec=pltpu.PrefetchScalarGridSpec(
            num_scalar_prefetch=3,
            grid=(block_count,),
            in_specs=[
                pl.BlockSpec((1, BLK, width), lambda b, *_: (b, 0, 0)),
            ] + [whole] * len(tables),
            out_specs=pl.BlockSpec((1, BLK, width), lambda b, *_: (b, 0, 0)),
            scratch_shapes=[
                pltpu.VMEM((keys, 2 * width), jnp.bfloat16),
            ],
        ),
        compiler_params=pltpu.CompilerParams(vmem_limit_bytes=60 * 1024 * 1024),
        cost_estimate=pl.CostEstimate(
            flops=4 * block_count * BLK * keys * width,
            transcendentals=block_count * heads * BLK * keys,
            bytes_accessed=sum(t.size * t.dtype.itemsize for t in tables) + 2 * queries.size * 2,
        ),
    )(count, source, rows, queries, *tables)


def project_kv(x, kv_w):
    return jnp.dot(x, kv_w, preferred_element_type=jnp.float32).astype(jnp.bfloat16)


def window_of(x, axis):
    parts = []
    for offset in (2, 1, 0, -1, -2):
        parts.append(x if offset == 0 else shifted(x, "seq", offset))
    return parts


def shards(tokens, w_qkv, w_out, neighbours, near_count, anchors):
    head_count = lax.axis_size("head")
    head_rank = lax.axis_index("head")
    width_here = D // head_count
    own_rows = tokens.shape[0]
    own_blocks = own_rows // BLK
    row_count = own_rows * head_count
    block_count = row_count // BLK
    neigh = neighbours.shape[1]
    col_start = head_rank * width_here
    query_w = lax.dynamic_slice_in_dim(w_qkv[:, 0], col_start, width_here, 1)
    key_w = lax.dynamic_slice_in_dim(w_qkv[:, 1], col_start, width_here, 1)
    value_w = lax.dynamic_slice_in_dim(w_qkv[:, 2], col_start, width_here, 1)

    kv_w = jnp.concatenate([key_w, value_w], axis=1)
    kva = window_of(project_kv(tokens, kv_w), 0)

    gathered = lax.all_gather(tokens, "head", axis=0, tiled=True)
    rest_tokens = jnp.roll(gathered, -head_rank * own_rows, axis=0)[own_rows:]
    kvb = window_of(project_kv(rest_tokens, kv_w), 0)
    rolled_tokens = jnp.concatenate([tokens, rest_tokens], axis=0)
    queries = jnp.dot(rolled_tokens, query_w, preferred_element_type=jnp.float32).astype(
        jnp.bfloat16
    ).reshape(block_count, BLK, width_here)

    seq_count = lax.axis_size("seq")
    seq_rank = lax.axis_index("seq")
    kvanc = gather_all(project_kv(gathered[:BLK], kv_w), "seq")
    held_count = kvanc.shape[0]
    kvanc = kvanc.reshape(held_count * BLK, 2 * width_here)
    first_block = (seq_rank - 2) * block_count

    shift = -head_rank * own_blocks
    neighbours = jnp.roll(neighbours, shift, axis=0)
    near_count = jnp.roll(near_count, shift, axis=0)
    anchors = jnp.roll(anchors, shift, axis=0)

    rel = jnp.clip(neighbours - first_block, 0, 5 * block_count - 1)
    offset_idx = rel // block_count
    within = rel % block_count
    chunk = within // own_blocks
    inner = within % own_blocks
    mine = chunk == head_rank
    row_b = ((chunk - head_rank) % head_count - 1) * own_blocks + inner
    near_row = jnp.where(mine, inner, row_b)
    offsets = len(kva)
    near_src = jnp.where(mine, 0, offsets) + offset_idx
    owner = jnp.clip(anchors // block_count, 0, seq_count - 1)
    anch_row = (owner - seq_rank + held_count - 1) % seq_count
    near_used = jnp.arange(neigh)[None, :] < near_count[:, None]
    repeated = jnp.any(
        (anchors[:, :, None] == neighbours[:, None, :]) & near_used[:, None, :], axis=2
    )
    valid = jnp.concatenate([near_used, jnp.logical_not(repeated)], axis=1)
    order = jnp.argsort(jnp.logical_not(valid).astype(jnp.int32), axis=1, stable=True)
    every_row = jnp.concatenate([near_row, anch_row], axis=1)
    every_src = jnp.concatenate([near_src, jnp.full_like(anch_row, 2 * offsets)], axis=1)
    rows = jnp.take_along_axis(every_row, order, axis=1).astype(jnp.int32)
    source = jnp.take_along_axis(every_src, order, axis=1).astype(jnp.int32)
    count = jnp.sum(valid.astype(jnp.int32), axis=1).astype(jnp.int32)

    tables = tuple(kva) + tuple(kvb) + (kvanc,)
    away = attention(queries[own_blocks:], tables, count[own_blocks:], source[own_blocks:],
                     rows[own_blocks:])
    away = away.reshape(head_count - 1, own_rows, width_here)
    received = [None] * head_count
    for j in range(1, head_count):
        pairs = [(z, (z + j) % head_count) for z in range(head_count)]
        received[j] = lax.ppermute(away[j - 1], "head", pairs)
    received[0] = attention(queries[:own_blocks], tables, count[:own_blocks],
                            source[:own_blocks], rows[:own_blocks]).reshape(own_rows, width_here)
    mine_rows = jnp.concatenate(received, axis=1)
    groups = (head_rank - jnp.arange(head_count)) % head_count
    out_w = jnp.take(w_out.reshape(head_count, width_here, D), groups, axis=0).reshape(D, D)
    mixed_out = jnp.dot(mine_rows, out_w, preferred_element_type=jnp.float32).astype(
        jnp.bfloat16
    )
    return mixed_out


def solution(mesh):
    placed = (P(("seq", "head"), None), P(), P(), P("seq", None), P("seq"), P("seq", None))
    return jax.shard_map(
        shards, mesh=mesh, in_specs=placed, out_specs=P(("seq", "head"), None), check_vma=False
    )
```

```python
import functools

import jax
import jax.numpy as jnp
from jax import lax
from jax.experimental import pallas as pl
from jax.experimental.pallas import tpu as pltpu
from jax.sharding import PartitionSpec as P

D = 768
HDIM = 64
BLK = 128


def shifted(x, axis, by):
    size = lax.axis_size(axis)
    pairs = [(i, i + by) for i in range(size) if 0 <= i + by < size]
    return lax.ppermute(x, axis, pairs)


def gather_all(x, axis):
    size = lax.axis_size(axis)
    rank = lax.axis_index(axis)
    held = x[None]
    step = 1
    while step < size:
        pairs = [(i, (i + step) % size) for i in range(size)]
        got = lax.ppermute(held, axis, pairs)
        held = jnp.concatenate([got, held], axis=0)
        step *= 2
    return held


def attention_kernel(count, source, rows, q_ref, *refs, heads, widths, scale):
    tables = refs[:-2]
    o_ref, kv_ref = refs[-2:]
    b = pl.program_id(0)
    used = count[b]

    @pl.when(b == 0)
    def _():
        kv_ref[...] = jnp.zeros_like(kv_ref)

    def fetch(j, carry):
        at = pl.multiple_of(j * BLK, BLK)
        row = rows[b, j]
        for code in range(len(tables)):
            @pl.when(source[b, j] == code)
            def _():
                start = pl.multiple_of(row * BLK, BLK)
                kv_ref[pl.ds(at, BLK), :] = tables[code][pl.ds(start, BLK), :]

        return carry

    lax.fori_loop(0, used, fetch, 0)
    limit = used * BLK

    width = heads * HDIM

    def run(slots):
        span = slots * BLK
        lane = lax.broadcasted_iota(jnp.int32, (1, span), 1)
        bias = jnp.where(lane < limit, 0.0, -jnp.inf)
        for h in range(heads):
            cols = slice(h * HDIM, (h + 1) * HDIM)
            qh = (q_ref[0, :, cols].astype(jnp.float32) * scale).astype(jnp.bfloat16)
            s = lax.dot_general(qh, kv_ref[0:span, cols], (((1,), (1,)), ((), ())),
                                preferred_element_type=jnp.float32) + bias
            peak = jnp.max(s, axis=-1, keepdims=True)
            e = jnp.exp(s - peak)
            totals = jnp.sum(e, axis=-1, keepdims=True)
            vcols = slice(width + h * HDIM, width + (h + 1) * HDIM)
            summed = jnp.dot(e.astype(jnp.bfloat16), kv_ref[0:span, vcols],
                             preferred_element_type=jnp.float32)
            o_ref[0, :, cols] = (summed / totals).astype(o_ref.dtype)

    low = 0
    for slots in widths:
        @pl.when((used > low) & (used <= slots))
        def _():
            run(slots)
        low = slots


def attention(queries, tables, count, source, rows, widths=None):
    block_count, _, width = queries.shape
    heads = width // HDIM
    slots = rows.shape[1]
    if widths is None:
        widths = tuple(w for w in (8, 12, 16) if w < slots) + (slots,)
    kernel = functools.partial(attention_kernel, heads=heads, widths=widths,
                               scale=HDIM ** (-0.5))
    whole = pl.BlockSpec(memory_space=pltpu.VMEM)
    keys = slots * BLK
    return pl.pallas_call(
        kernel,
        out_shape=jax.ShapeDtypeStruct(queries.shape, jnp.bfloat16),
        grid_spec=pltpu.PrefetchScalarGridSpec(
            num_scalar_prefetch=3,
            grid=(block_count,),
            in_specs=[
                pl.BlockSpec((1, BLK, width), lambda b, *_: (b, 0, 0)),
            ] + [whole] * len(tables),
            out_specs=pl.BlockSpec((1, BLK, width), lambda b, *_: (b, 0, 0)),
            scratch_shapes=[
                pltpu.VMEM((keys, 2 * width), jnp.bfloat16),
            ],
        ),
        compiler_params=pltpu.CompilerParams(vmem_limit_bytes=60 * 1024 * 1024),
        cost_estimate=pl.CostEstimate(
            flops=4 * block_count * BLK * keys * width,
            transcendentals=block_count * heads * BLK * keys,
            bytes_accessed=sum(t.size * t.dtype.itemsize for t in tables) + 2 * queries.size * 2,
        ),
    )(count, source, rows, queries, *tables)


def project_kv(x, kv_w):
    return jnp.dot(x, kv_w, preferred_element_type=jnp.float32).astype(jnp.bfloat16)


def window_of(x, axis):
    size = lax.axis_size("seq")
    plus1 = shifted(x, "seq", 1)
    minus1 = shifted(x, "seq", -1)
    plus2 = lax.ppermute(x, "seq", [(i, i + 2) for i in range(0, size - 2, 2)])
    plus2 = plus2 + lax.ppermute(plus1, "seq", [(i, i + 1) for i in range(2, size, 2)])
    minus2 = lax.ppermute(x, "seq", [(i, i - 2) for i in range(3, size, 2)])
    minus2 = minus2 + lax.ppermute(minus1, "seq", [(i, i - 1) for i in range(1, size - 2, 2)])
    return jnp.concatenate([plus2, plus1, x, minus1, minus2], axis=axis)


def shards(tokens, w_qkv, w_out, neighbours, near_count, anchors):
    head_count = lax.axis_size("head")
    head_rank = lax.axis_index("head")
    width_here = D // head_count
    own_rows = tokens.shape[0]
    own_blocks = own_rows // BLK
    row_count = own_rows * head_count
    block_count = row_count // BLK
    neigh = neighbours.shape[1]
    col_start = head_rank * width_here
    query_w = lax.dynamic_slice_in_dim(w_qkv[:, 0], col_start, width_here, 1)
    key_w = lax.dynamic_slice_in_dim(w_qkv[:, 1], col_start, width_here, 1)
    value_w = lax.dynamic_slice_in_dim(w_qkv[:, 2], col_start, width_here, 1)

    kv_w = jnp.concatenate([key_w, value_w], axis=1)
    kva = window_of(project_kv(tokens, kv_w), 0)

    gathered = lax.all_gather(tokens, "head", axis=0, tiled=True)
    rest_tokens = jnp.roll(gathered, -head_rank * own_rows, axis=0)[own_rows:]
    kvb = window_of(project_kv(rest_tokens, kv_w), 0)
    rolled_tokens = jnp.concatenate([tokens, rest_tokens], axis=0)
    queries = jnp.dot(rolled_tokens, query_w, preferred_element_type=jnp.float32).astype(
        jnp.bfloat16
    ).reshape(block_count, BLK, width_here)

    seq_count = lax.axis_size("seq")
    seq_rank = lax.axis_index("seq")
    kvanc = gather_all(project_kv(gathered[:BLK], kv_w), "seq")
    held_count = kvanc.shape[0]
    kvanc = kvanc.reshape(held_count * BLK, 2 * width_here)
    first_block = (seq_rank - 2) * block_count

    shift = -head_rank * own_blocks
    neighbours = jnp.roll(neighbours, shift, axis=0)
    near_count = jnp.roll(near_count, shift, axis=0)
    anchors = jnp.roll(anchors, shift, axis=0)

    rel = jnp.clip(neighbours - first_block, 0, 5 * block_count - 1)
    offset_idx = rel // block_count
    within = rel % block_count
    chunk = within // own_blocks
    inner = within % own_blocks
    mine = chunk == head_rank
    row_a = offset_idx * own_blocks + inner
    row_b = (offset_idx * (block_count - own_blocks)
             + ((chunk - head_rank) % head_count - 1) * own_blocks + inner)
    near_row = jnp.where(mine, row_a, row_b)
    near_src = jnp.where(mine, 0, 1)
    owner = jnp.clip(anchors // block_count, 0, seq_count - 1)
    anch_row = (owner - seq_rank + held_count - 1) % seq_count
    near_used = jnp.arange(neigh)[None, :] < near_count[:, None]
    repeated = jnp.any(
        (anchors[:, :, None] == neighbours[:, None, :]) & near_used[:, None, :], axis=2
    )
    valid = jnp.concatenate([near_used, jnp.logical_not(repeated)], axis=1)
    order = jnp.argsort(jnp.logical_not(valid).astype(jnp.int32), axis=1, stable=True)
    every_row = jnp.concatenate([near_row, anch_row], axis=1)
    every_src = jnp.concatenate([near_src, jnp.full_like(anch_row, 2)], axis=1)
    rows = jnp.take_along_axis(every_row, order, axis=1).astype(jnp.int32)
    source = jnp.take_along_axis(every_src, order, axis=1).astype(jnp.int32)
    count = jnp.sum(valid.astype(jnp.int32), axis=1).astype(jnp.int32)

    tables = (kva, kvb, kvanc)
    away = attention(queries[own_blocks:], tables, count[own_blocks:], source[own_blocks:],
                     rows[own_blocks:])
    away = away.reshape(head_count - 1, own_rows, width_here)
    received = [None] * head_count
    for j in range(1, head_count):
        pairs = [(z, (z + j) % head_count) for z in range(head_count)]
        received[j] = lax.ppermute(away[j - 1], "head", pairs)
    received[0] = attention(queries[:own_blocks], tables, count[:own_blocks],
                            source[:own_blocks], rows[:own_blocks]).reshape(own_rows, width_here)
    mine_rows = jnp.concatenate(received, axis=1)
    groups = (head_rank - jnp.arange(head_count)) % head_count
    out_w = jnp.take(w_out.reshape(head_count, width_here, D), groups, axis=0).reshape(D, D)
    mixed_out = jnp.dot(mine_rows, out_w, preferred_element_type=jnp.float32).astype(
        jnp.bfloat16
    )
    return mixed_out


def solution(mesh):
    placed = (P(("seq", "head"), None), P(), P(), P("seq", None), P("seq"), P("seq", None))
    return jax.shard_map(
        shards, mesh=mesh, in_specs=placed, out_specs=P(("seq", "head"), None), check_vma=False
    )
```

```python
import functools

import jax
import jax.numpy as jnp
from jax import lax
from jax.experimental import pallas as pl
from jax.experimental.pallas import tpu as pltpu
from jax.sharding import PartitionSpec as P

D = 768
HDIM = 64
BLK = 128


def shifted(x, axis, by):
    size = lax.axis_size(axis)
    pairs = [(i, i + by) for i in range(size) if 0 <= i + by < size]
    return lax.ppermute(x, axis, pairs)


def gather_all(x, axis):
    size = lax.axis_size(axis)
    rank = lax.axis_index(axis)
    held = x[None]
    step = 1
    while step < size:
        pairs = [(i, (i + step) % size) for i in range(size)]
        got = lax.ppermute(held, axis, pairs)
        held = jnp.concatenate([got, held], axis=0)
        step *= 2
    return held


def attention_kernel(count, source, rows, q_ref, *refs, heads, widths, scale):
    tables = refs[:-2]
    o_ref, kv_ref = refs[-2:]
    b = pl.program_id(0)
    used = count[b]

    @pl.when(b == 0)
    def _():
        kv_ref[...] = jnp.zeros_like(kv_ref)

    def fetch(j, carry):
        at = pl.multiple_of(j * BLK, BLK)
        row = rows[b, j]
        for code in range(len(tables)):
            @pl.when(source[b, j] == code)
            def _():
                start = pl.multiple_of(row * BLK, BLK)
                kv_ref[pl.ds(at, BLK), :] = tables[code][pl.ds(start, BLK), :]

        return carry

    lax.fori_loop(0, used, fetch, 0)
    limit = used * BLK

    width = heads * HDIM

    def run(slots):
        span = slots * BLK
        lane = lax.broadcasted_iota(jnp.int32, (1, span), 1)
        bias = jnp.where(lane < limit, 0.0, -jnp.inf)
        for h in range(heads):
            cols = slice(h * HDIM, (h + 1) * HDIM)
            qh = (q_ref[0, :, cols].astype(jnp.float32) * scale).astype(jnp.bfloat16)
            s = lax.dot_general(qh, kv_ref[0:span, cols], (((1,), (1,)), ((), ())),
                                preferred_element_type=jnp.float32) + bias
            peak = jnp.max(s, axis=-1, keepdims=True)
            e = jnp.exp(s - peak)
            totals = jnp.sum(e, axis=-1, keepdims=True)
            vcols = slice(width + h * HDIM, width + (h + 1) * HDIM)
            summed = jnp.dot(e.astype(jnp.bfloat16), kv_ref[0:span, vcols],
                             preferred_element_type=jnp.float32)
            o_ref[0, :, cols] = (summed / totals).astype(o_ref.dtype)

    low = 0
    for slots in widths:
        @pl.when((used > low) & (used <= slots))
        def _():
            run(slots)
        low = slots


def attention(queries, tables, count, source, rows, widths=None):
    block_count, _, width = queries.shape
    heads = width // HDIM
    slots = rows.shape[1]
    if widths is None:
        widths = tuple(w for w in (8, 12, 16) if w < slots) + (slots,)
    kernel = functools.partial(attention_kernel, heads=heads, widths=widths,
                               scale=HDIM ** (-0.5))
    whole = pl.BlockSpec(memory_space=pltpu.VMEM)
    keys = slots * BLK
    return pl.pallas_call(
        kernel,
        out_shape=jax.ShapeDtypeStruct(queries.shape, jnp.bfloat16),
        grid_spec=pltpu.PrefetchScalarGridSpec(
            num_scalar_prefetch=3,
            grid=(block_count,),
            in_specs=[
                pl.BlockSpec((1, BLK, width), lambda b, *_: (b, 0, 0)),
            ] + [whole] * len(tables),
            out_specs=pl.BlockSpec((1, BLK, width), lambda b, *_: (b, 0, 0)),
            scratch_shapes=[
                pltpu.VMEM((keys, 2 * width), jnp.bfloat16),
            ],
        ),
        compiler_params=pltpu.CompilerParams(vmem_limit_bytes=60 * 1024 * 1024),
        cost_estimate=pl.CostEstimate(
            flops=4 * block_count * BLK * keys * width,
            transcendentals=block_count * heads * BLK * keys,
            bytes_accessed=sum(t.size * t.dtype.itemsize for t in tables) + 2 * queries.size * 2,
        ),
    )(count, source, rows, queries, *tables)


def project_kv(x, kv_w):
    return jnp.dot(x, kv_w, preferred_element_type=jnp.float32).astype(jnp.bfloat16)


def window_of(x, axis):
    parts = []
    for offset in (2, 1, 0, -1, -2):
        parts.append(x if offset == 0 else shifted(x, "seq", offset))
    return jnp.concatenate(parts, axis=axis)


def shards(tokens, w_qkv, w_out, neighbours, near_count, anchors):
    head_count = lax.axis_size("head")
    head_rank = lax.axis_index("head")
    width_here = D // head_count
    own_rows = tokens.shape[0]
    own_blocks = own_rows // BLK
    row_count = own_rows * head_count
    block_count = row_count // BLK
    neigh = neighbours.shape[1]
    col_start = head_rank * width_here
    query_w = lax.dynamic_slice_in_dim(w_qkv[:, 0], col_start, width_here, 1)
    key_w = lax.dynamic_slice_in_dim(w_qkv[:, 1], col_start, width_here, 1)
    value_w = lax.dynamic_slice_in_dim(w_qkv[:, 2], col_start, width_here, 1)

    kv_w = jnp.concatenate([key_w, value_w], axis=1)
    kva = window_of(project_kv(tokens, kv_w), 0)

    rest_tokens = jnp.concatenate(
        [
            lax.ppermute(tokens, "head", [(z, (z - k) % head_count) for z in range(head_count)])
            for k in range(1, head_count)
        ],
        axis=0,
    )
    kvb = window_of(project_kv(rest_tokens, kv_w), 0)
    rolled_tokens = jnp.concatenate([tokens, rest_tokens], axis=0)
    queries = jnp.dot(rolled_tokens, query_w, preferred_element_type=jnp.float32).astype(
        jnp.bfloat16
    ).reshape(block_count, BLK, width_here)

    seq_count = lax.axis_size("seq")
    seq_rank = lax.axis_index("seq")
    first_at = ((head_count - head_rank) % head_count) * own_rows
    first_rows = lax.dynamic_slice_in_dim(rolled_tokens, first_at, BLK, 0)
    kvanc = gather_all(project_kv(first_rows, kv_w), "seq")
    held_count = kvanc.shape[0]
    kvanc = kvanc.reshape(held_count * BLK, 2 * width_here)
    first_block = (seq_rank - 2) * block_count

    shift = -head_rank * own_blocks
    neighbours = jnp.roll(neighbours, shift, axis=0)
    near_count = jnp.roll(near_count, shift, axis=0)
    anchors = jnp.roll(anchors, shift, axis=0)

    rel = jnp.clip(neighbours - first_block, 0, 5 * block_count - 1)
    offset_idx = rel // block_count
    within = rel % block_count
    chunk = within // own_blocks
    inner = within % own_blocks
    mine = chunk == head_rank
    row_a = offset_idx * own_blocks + inner
    row_b = (offset_idx * (block_count - own_blocks)
             + ((chunk - head_rank) % head_count - 1) * own_blocks + inner)
    near_row = jnp.where(mine, row_a, row_b)
    near_src = jnp.where(mine, 0, 1)
    owner = jnp.clip(anchors // block_count, 0, seq_count - 1)
    anch_row = (owner - seq_rank + held_count - 1) % seq_count
    near_used = jnp.arange(neigh)[None, :] < near_count[:, None]
    repeated = jnp.any(
        (anchors[:, :, None] == neighbours[:, None, :]) & near_used[:, None, :], axis=2
    )
    valid = jnp.concatenate([near_used, jnp.logical_not(repeated)], axis=1)
    order = jnp.argsort(jnp.logical_not(valid).astype(jnp.int32), axis=1, stable=True)
    every_row = jnp.concatenate([near_row, anch_row], axis=1)
    every_src = jnp.concatenate([near_src, jnp.full_like(anch_row, 2)], axis=1)
    rows = jnp.take_along_axis(every_row, order, axis=1).astype(jnp.int32)
    source = jnp.take_along_axis(every_src, order, axis=1).astype(jnp.int32)
    count = jnp.sum(valid.astype(jnp.int32), axis=1).astype(jnp.int32)

    tables = (kva, kvb, kvanc)
    away = attention(queries[own_blocks:], tables, count[own_blocks:], source[own_blocks:],
                     rows[own_blocks:])
    away = away.reshape(head_count - 1, own_rows, width_here)
    received = [None] * head_count
    for j in range(1, head_count):
        pairs = [(z, (z + j) % head_count) for z in range(head_count)]
        received[j] = lax.ppermute(away[j - 1], "head", pairs)
    received[0] = attention(queries[:own_blocks], tables, count[:own_blocks],
                            source[:own_blocks], rows[:own_blocks]).reshape(own_rows, width_here)
    mine_rows = jnp.concatenate(received, axis=1)
    groups = (head_rank - jnp.arange(head_count)) % head_count
    out_w = jnp.take(w_out.reshape(head_count, width_here, D), groups, axis=0).reshape(D, D)
    mixed_out = jnp.dot(mine_rows, out_w, preferred_element_type=jnp.float32).astype(
        jnp.bfloat16
    )
    return mixed_out


def solution(mesh):
    placed = (P(("seq", "head"), None), P(), P(), P("seq", None), P("seq"), P("seq", None))
    return jax.shard_map(
        shards, mesh=mesh, in_specs=placed, out_specs=P(("seq", "head"), None), check_vma=False
    )
```

```python
import functools

import jax
import jax.numpy as jnp
from jax import lax
from jax.experimental import pallas as pl
from jax.experimental.pallas import tpu as pltpu
from jax.sharding import PartitionSpec as P

D = 768
HDIM = 64
BLK = 128


def shifted(x, axis, by):
    size = lax.axis_size(axis)
    pairs = [(i, i + by) for i in range(size) if 0 <= i + by < size]
    return lax.ppermute(x, axis, pairs)


def gather_all(x, axis):
    size = lax.axis_size(axis)
    rank = lax.axis_index(axis)
    held = x[None]
    step = 1
    while step < size:
        pairs = [(i, (i + step) % size) for i in range(size)]
        got = lax.ppermute(held, axis, pairs)
        held = jnp.concatenate([got, held], axis=0)
        step *= 2
    return held


def attention_kernel(count, source, rows, q_ref, *refs, heads, widths, scale):
    tables = refs[:-2]
    o_ref, kv_ref = refs[-2:]
    b = pl.program_id(0)
    used = count[b]

    @pl.when(b == 0)
    def _():
        kv_ref[...] = jnp.zeros_like(kv_ref)

    def fetch(j, carry):
        at = pl.multiple_of(j * BLK, BLK)
        row = rows[b, j]
        for code in range(len(tables)):
            @pl.when(source[b, j] == code)
            def _():
                start = pl.multiple_of(row * BLK, BLK)
                kv_ref[pl.ds(at, BLK), :] = tables[code][pl.ds(start, BLK), :]

        return carry

    lax.fori_loop(0, used, fetch, 0)
    limit = used * BLK

    width = heads * HDIM

    def run(slots):
        span = slots * BLK
        lane = lax.broadcasted_iota(jnp.int32, (1, span), 1)
        bias = jnp.where(lane < limit, 0.0, -jnp.inf)
        for h in range(heads):
            cols = slice(h * HDIM, (h + 1) * HDIM)
            qh = (q_ref[0, :, cols].astype(jnp.float32) * scale).astype(jnp.bfloat16)
            s = lax.dot_general(qh, kv_ref[0:span, cols], (((1,), (1,)), ((), ())),
                                preferred_element_type=jnp.float32) + bias
            peak = jnp.max(s, axis=-1, keepdims=True)
            e = jnp.exp(s - peak)
            totals = jnp.sum(e, axis=-1, keepdims=True)
            vcols = slice(width + h * HDIM, width + (h + 1) * HDIM)
            summed = jnp.dot(e.astype(jnp.bfloat16), kv_ref[0:span, vcols],
                             preferred_element_type=jnp.float32)
            o_ref[0, :, cols] = (summed / totals).astype(o_ref.dtype)

    low = 0
    for slots in widths:
        @pl.when((used > low) & (used <= slots))
        def _():
            run(slots)
        low = slots


def attention(queries, tables, count, source, rows, widths=None):
    block_count, _, width = queries.shape
    heads = width // HDIM
    slots = rows.shape[1]
    if widths is None:
        widths = tuple(w for w in (8, 12, 16) if w < slots) + (slots,)
    kernel = functools.partial(attention_kernel, heads=heads, widths=widths,
                               scale=HDIM ** (-0.5))
    whole = pl.BlockSpec(memory_space=pltpu.VMEM)
    keys = slots * BLK
    return pl.pallas_call(
        kernel,
        out_shape=jax.ShapeDtypeStruct(queries.shape, jnp.bfloat16),
        grid_spec=pltpu.PrefetchScalarGridSpec(
            num_scalar_prefetch=3,
            grid=(block_count,),
            in_specs=[
                pl.BlockSpec((1, BLK, width), lambda b, *_: (b, 0, 0)),
            ] + [whole] * len(tables),
            out_specs=pl.BlockSpec((1, BLK, width), lambda b, *_: (b, 0, 0)),
            scratch_shapes=[
                pltpu.VMEM((keys, 2 * width), jnp.bfloat16),
            ],
        ),
        compiler_params=pltpu.CompilerParams(vmem_limit_bytes=60 * 1024 * 1024),
        cost_estimate=pl.CostEstimate(
            flops=4 * block_count * BLK * keys * width,
            transcendentals=block_count * heads * BLK * keys,
            bytes_accessed=sum(t.size * t.dtype.itemsize for t in tables) + 2 * queries.size * 2,
        ),
    )(count, source, rows, queries, *tables)


def project_kv(x, kv_w):
    return jnp.dot(x, kv_w, preferred_element_type=jnp.float32).astype(jnp.bfloat16)


def window_of(x, axis):
    parts = []
    for offset in (2, 1, 0, -1, -2):
        parts.append(x if offset == 0 else shifted(x, "seq", offset))
    return jnp.concatenate(parts, axis=axis)


def shards(tokens, w_qkv, w_out, neighbours, near_count, anchors):
    head_count = lax.axis_size("head")
    head_rank = lax.axis_index("head")
    width_here = D // head_count
    own_rows = tokens.shape[0]
    own_blocks = own_rows // BLK
    row_count = own_rows * head_count
    block_count = row_count // BLK
    neigh = neighbours.shape[1]
    col_start = head_rank * width_here
    query_w = lax.dynamic_slice_in_dim(w_qkv[:, 0], col_start, width_here, 1)
    key_w = lax.dynamic_slice_in_dim(w_qkv[:, 1], col_start, width_here, 1)
    value_w = lax.dynamic_slice_in_dim(w_qkv[:, 2], col_start, width_here, 1)

    kv_w = jnp.concatenate([key_w, value_w], axis=1)
    kva = window_of(project_kv(tokens, kv_w), 0)

    def fetch_chunk(source, k):
        pairs = [(z, (z - k) % head_count) for z in range(head_count)]
        return lax.ppermute(source, "head", pairs)

    near_k = sorted({1, head_count - 1})
    groups = [near_k] + ([[k for k in range(1, head_count) if k not in near_k]]
                         if head_count > 3 else [])
    group_of, slot_of, size_of = [0] * head_count, [0] * head_count, [0] * head_count
    kv_groups = []
    received = {}
    source = tokens
    for g, members in enumerate(groups):
        for p, k in enumerate(members):
            group_of[k], slot_of[k], size_of[k] = g, p, len(members)
            received[k] = fetch_chunk(source, k)
        kv = project_kv(jnp.concatenate([received[k] for k in members], axis=0), kv_w)
        source, kv = lax.optimization_barrier((tokens, kv))
        kv_groups.append(window_of(kv, 0))
    rest_tokens = jnp.concatenate([received[k] for k in range(1, head_count)], axis=0)
    rolled_tokens = jnp.concatenate([tokens, rest_tokens], axis=0)
    queries = jnp.dot(rolled_tokens, query_w, preferred_element_type=jnp.float32).astype(
        jnp.bfloat16
    ).reshape(block_count, BLK, width_here)

    seq_count = lax.axis_size("seq")
    seq_rank = lax.axis_index("seq")
    first_at = ((head_count - head_rank) % head_count) * own_rows
    first_rows = lax.dynamic_slice_in_dim(rolled_tokens, first_at, BLK, 0)
    kvanc = gather_all(project_kv(first_rows, kv_w), "seq")
    held_count = kvanc.shape[0]
    kvanc = kvanc.reshape(held_count * BLK, 2 * width_here)
    first_block = (seq_rank - 2) * block_count

    shift = -head_rank * own_blocks
    neighbours = jnp.roll(neighbours, shift, axis=0)
    near_count = jnp.roll(near_count, shift, axis=0)
    anchors = jnp.roll(anchors, shift, axis=0)

    rel = jnp.clip(neighbours - first_block, 0, 5 * block_count - 1)
    offset_idx = rel // block_count
    within = rel % block_count
    chunk = within // own_blocks
    inner = within % own_blocks
    mine = chunk == head_rank
    row_a = offset_idx * own_blocks + inner
    hop = (chunk - head_rank) % head_count
    hop_group = jnp.asarray(group_of, jnp.int32)[hop]
    hop_slot = jnp.asarray(slot_of, jnp.int32)[hop]
    hop_size = jnp.asarray(size_of, jnp.int32)[hop]
    row_b = (offset_idx * hop_size + hop_slot) * own_blocks + inner
    near_row = jnp.where(mine, row_a, row_b)
    near_src = jnp.where(mine, 0, 1 + hop_group)
    owner = jnp.clip(anchors // block_count, 0, seq_count - 1)
    anch_row = (owner - seq_rank + held_count - 1) % seq_count
    near_used = jnp.arange(neigh)[None, :] < near_count[:, None]
    repeated = jnp.any(
        (anchors[:, :, None] == neighbours[:, None, :]) & near_used[:, None, :], axis=2
    )
    valid = jnp.concatenate([near_used, jnp.logical_not(repeated)], axis=1)
    order = jnp.argsort(jnp.logical_not(valid).astype(jnp.int32), axis=1, stable=True)
    every_row = jnp.concatenate([near_row, anch_row], axis=1)
    every_src = jnp.concatenate([near_src, jnp.full_like(anch_row, 1 + len(groups))], axis=1)
    rows = jnp.take_along_axis(every_row, order, axis=1).astype(jnp.int32)
    source = jnp.take_along_axis(every_src, order, axis=1).astype(jnp.int32)
    count = jnp.sum(valid.astype(jnp.int32), axis=1).astype(jnp.int32)

    tables = (kva, *kv_groups, kvanc)
    away = attention(queries[own_blocks:], tables, count[own_blocks:], source[own_blocks:],
                     rows[own_blocks:])
    away = away.reshape(head_count - 1, own_rows, width_here)
    received = [None] * head_count
    for j in range(1, head_count):
        pairs = [(z, (z + j) % head_count) for z in range(head_count)]
        received[j] = lax.ppermute(away[j - 1], "head", pairs)
    received[0] = attention(queries[:own_blocks], tables, count[:own_blocks],
                            source[:own_blocks], rows[:own_blocks]).reshape(own_rows, width_here)
    mine_rows = jnp.concatenate(received, axis=1)
    groups = (head_rank - jnp.arange(head_count)) % head_count
    out_w = jnp.take(w_out.reshape(head_count, width_here, D), groups, axis=0).reshape(D, D)
    mixed_out = jnp.dot(mine_rows, out_w, preferred_element_type=jnp.float32).astype(
        jnp.bfloat16
    )
    return mixed_out


def solution(mesh):
    placed = (P(("seq", "head"), None), P(), P(), P("seq", None), P("seq"), P("seq", None))
    return jax.shard_map(
        shards, mesh=mesh, in_specs=placed, out_specs=P(("seq", "head"), None), check_vma=False
    )
```

```python
import functools

import jax
import jax.numpy as jnp
from jax import lax
from jax.experimental import pallas as pl
from jax.experimental.pallas import tpu as pltpu
from jax.sharding import PartitionSpec as P

D = 768
HDIM = 64
BLK = 128


def shifted(x, axis, by):
    size = lax.axis_size(axis)
    pairs = [(i, i + by) for i in range(size) if 0 <= i + by < size]
    return lax.ppermute(x, axis, pairs)


def gather_all(x, axis):
    size = lax.axis_size(axis)
    rank = lax.axis_index(axis)
    held = x[None]
    step = 1
    while step < size:
        pairs = [(i, (i + step) % size) for i in range(size)]
        got = lax.ppermute(held, axis, pairs)
        held = jnp.concatenate([got, held], axis=0)
        step *= 2
    return held


def attention_kernel(count, source, rows, q_ref, *refs, heads, widths, scale):
    tables = refs[:-2]
    o_ref, kv_ref = refs[-2:]
    b = pl.program_id(0)
    used = count[b]

    @pl.when(b == 0)
    def _():
        kv_ref[...] = jnp.zeros_like(kv_ref)

    def fetch(j, carry):
        at = pl.multiple_of(j * BLK, BLK)
        row = rows[b, j]
        for code in range(len(tables)):
            @pl.when(source[b, j] == code)
            def _():
                start = pl.multiple_of(row * BLK, BLK)
                kv_ref[pl.ds(at, BLK), :] = tables[code][pl.ds(start, BLK), :]

        return carry

    lax.fori_loop(0, used, fetch, 0)
    limit = used * BLK

    width = heads * HDIM

    def run(slots):
        span = slots * BLK
        lane = lax.broadcasted_iota(jnp.int32, (1, span), 1)
        bias = jnp.where(lane < limit, 0.0, -jnp.inf)
        for h in range(heads):
            cols = slice(h * HDIM, (h + 1) * HDIM)
            qh = (q_ref[0, :, cols].astype(jnp.float32) * scale).astype(jnp.bfloat16)
            s = lax.dot_general(qh, kv_ref[0:span, cols], (((1,), (1,)), ((), ())),
                                preferred_element_type=jnp.float32) + bias
            peak = jnp.max(s, axis=-1, keepdims=True)
            e = jnp.exp(s - peak)
            totals = jnp.sum(e, axis=-1, keepdims=True)
            vcols = slice(width + h * HDIM, width + (h + 1) * HDIM)
            summed = jnp.dot(e.astype(jnp.bfloat16), kv_ref[0:span, vcols],
                             preferred_element_type=jnp.float32)
            o_ref[0, :, cols] = (summed / totals).astype(o_ref.dtype)

    low = 0
    for slots in widths:
        @pl.when((used > low) & (used <= slots))
        def _():
            run(slots)
        low = slots


def attention(queries, tables, count, source, rows, widths=None):
    block_count, _, width = queries.shape
    heads = width // HDIM
    slots = rows.shape[1]
    if widths is None:
        widths = tuple(w for w in (8, 12, 16) if w < slots) + (slots,)
    kernel = functools.partial(attention_kernel, heads=heads, widths=widths,
                               scale=HDIM ** (-0.5))
    whole = pl.BlockSpec(memory_space=pltpu.VMEM)
    keys = slots * BLK
    return pl.pallas_call(
        kernel,
        out_shape=jax.ShapeDtypeStruct(queries.shape, jnp.bfloat16),
        grid_spec=pltpu.PrefetchScalarGridSpec(
            num_scalar_prefetch=3,
            grid=(block_count,),
            in_specs=[
                pl.BlockSpec((1, BLK, width), lambda b, *_: (b, 0, 0)),
            ] + [whole] * len(tables),
            out_specs=pl.BlockSpec((1, BLK, width), lambda b, *_: (b, 0, 0)),
            scratch_shapes=[
                pltpu.VMEM((keys, 2 * width), jnp.bfloat16),
            ],
        ),
        compiler_params=pltpu.CompilerParams(vmem_limit_bytes=60 * 1024 * 1024),
        cost_estimate=pl.CostEstimate(
            flops=4 * block_count * BLK * keys * width,
            transcendentals=block_count * heads * BLK * keys,
            bytes_accessed=sum(t.size * t.dtype.itemsize for t in tables) + 2 * queries.size * 2,
        ),
    )(count, source, rows, queries, *tables)


def project_kv(x, kv_w):
    return jnp.dot(x, kv_w, preferred_element_type=jnp.float32).astype(jnp.bfloat16)


def window_of(x, axis):
    parts = []
    for offset in (2, 1, 0, -1, -2):
        parts.append(x if offset == 0 else shifted(x, "seq", offset))
    return jnp.concatenate(parts, axis=axis)


def shards(tokens, w_qkv, w_out, neighbours, near_count, anchors):
    head_count = lax.axis_size("head")
    head_rank = lax.axis_index("head")
    width_here = D // head_count
    own_rows = tokens.shape[0]
    own_blocks = own_rows // BLK
    row_count = own_rows * head_count
    block_count = row_count // BLK
    neigh = neighbours.shape[1]
    col_start = head_rank * width_here
    query_w = lax.dynamic_slice_in_dim(w_qkv[:, 0], col_start, width_here, 1)
    key_w = lax.dynamic_slice_in_dim(w_qkv[:, 1], col_start, width_here, 1)
    value_w = lax.dynamic_slice_in_dim(w_qkv[:, 2], col_start, width_here, 1)

    kv_w = jnp.concatenate([key_w, value_w], axis=1)
    kva = window_of(project_kv(tokens, kv_w), 0)

    def fetch_chunk(source, k):
        pairs = [(z, (z - k) % head_count) for z in range(head_count)]
        return lax.ppermute(source, "head", pairs)

    near_k = sorted({1, head_count - 1})
    groups = [near_k] + ([[k for k in range(1, head_count) if k not in near_k]]
                         if head_count > 3 else [])
    group_of, slot_of, size_of = [0] * head_count, [0] * head_count, [0] * head_count
    kv_groups = []
    received = {}
    source = tokens
    for g, members in enumerate(groups):
        for p, k in enumerate(members):
            group_of[k], slot_of[k], size_of[k] = g, p, len(members)
            received[k] = fetch_chunk(source, k)
        kv = project_kv(jnp.concatenate([received[k] for k in members], axis=0), kv_w)
        source, kv = lax.optimization_barrier((tokens, kv))
        kv_groups.append(window_of(kv, 0))
    rest_tokens = jnp.concatenate([received[k] for k in range(1, head_count)], axis=0)
    rolled_tokens = jnp.concatenate([tokens, rest_tokens], axis=0)
    queries = jnp.dot(rolled_tokens, query_w, preferred_element_type=jnp.float32).astype(
        jnp.bfloat16
    ).reshape(block_count, BLK, width_here)

    seq_count = lax.axis_size("seq")
    seq_rank = lax.axis_index("seq")
    late = [k for members in groups[1:] for k in members]
    first_hop = (-head_rank) % head_count
    first_rows = tokens[:BLK]
    if late:
        early_first = lax.ppermute(tokens[:BLK], "head",
                                   [(0, (-k) % head_count) for k in late])
        for k in late:
            first_rows = jnp.where(first_hop == k, early_first, first_rows)
    for k in groups[0]:
        first_rows = jnp.where(first_hop == k, received[k][:BLK], first_rows)
    kvanc = gather_all(project_kv(first_rows, kv_w), "seq")
    held_count = kvanc.shape[0]
    kvanc = kvanc.reshape(held_count * BLK, 2 * width_here)
    first_block = (seq_rank - 2) * block_count

    shift = -head_rank * own_blocks
    neighbours = jnp.roll(neighbours, shift, axis=0)
    near_count = jnp.roll(near_count, shift, axis=0)
    anchors = jnp.roll(anchors, shift, axis=0)

    rel = jnp.clip(neighbours - first_block, 0, 5 * block_count - 1)
    offset_idx = rel // block_count
    within = rel % block_count
    chunk = within // own_blocks
    inner = within % own_blocks
    mine = chunk == head_rank
    row_a = offset_idx * own_blocks + inner
    hop = (chunk - head_rank) % head_count
    hop_group = jnp.asarray(group_of, jnp.int32)[hop]
    hop_slot = jnp.asarray(slot_of, jnp.int32)[hop]
    hop_size = jnp.asarray(size_of, jnp.int32)[hop]
    row_b = (offset_idx * hop_size + hop_slot) * own_blocks + inner
    near_row = jnp.where(mine, row_a, row_b)
    near_src = jnp.where(mine, 0, 1 + hop_group)
    owner = jnp.clip(anchors // block_count, 0, seq_count - 1)
    anch_row = (owner - seq_rank + held_count - 1) % seq_count
    near_used = jnp.arange(neigh)[None, :] < near_count[:, None]
    repeated = jnp.any(
        (anchors[:, :, None] == neighbours[:, None, :]) & near_used[:, None, :], axis=2
    )
    valid = jnp.concatenate([near_used, jnp.logical_not(repeated)], axis=1)
    order = jnp.argsort(jnp.logical_not(valid).astype(jnp.int32), axis=1, stable=True)
    every_row = jnp.concatenate([near_row, anch_row], axis=1)
    every_src = jnp.concatenate([near_src, jnp.full_like(anch_row, 1 + len(groups))], axis=1)
    rows = jnp.take_along_axis(every_row, order, axis=1).astype(jnp.int32)
    source = jnp.take_along_axis(every_src, order, axis=1).astype(jnp.int32)
    count = jnp.sum(valid.astype(jnp.int32), axis=1).astype(jnp.int32)

    tables = (kva, *kv_groups, kvanc)
    away = attention(queries[own_blocks:], tables, count[own_blocks:], source[own_blocks:],
                     rows[own_blocks:])
    away = away.reshape(head_count - 1, own_rows, width_here)
    received = [None] * head_count
    for j in range(1, head_count):
        pairs = [(z, (z + j) % head_count) for z in range(head_count)]
        received[j] = lax.ppermute(away[j - 1], "head", pairs)
    received[0] = attention(queries[:own_blocks], tables, count[:own_blocks],
                            source[:own_blocks], rows[:own_blocks]).reshape(own_rows, width_here)
    mine_rows = jnp.concatenate(received, axis=1)
    groups = (head_rank - jnp.arange(head_count)) % head_count
    out_w = jnp.take(w_out.reshape(head_count, width_here, D), groups, axis=0).reshape(D, D)
    mixed_out = jnp.dot(mine_rows, out_w, preferred_element_type=jnp.float32).astype(
        jnp.bfloat16
    )
    return mixed_out


def solution(mesh):
    placed = (P(("seq", "head"), None), P(), P(), P("seq", None), P("seq"), P("seq", None))
    return jax.shard_map(
        shards, mesh=mesh, in_specs=placed, out_specs=P(("seq", "head"), None), check_vma=False
    )
```

```python
import functools

import jax
import jax.numpy as jnp
from jax import lax
from jax.experimental import pallas as pl
from jax.experimental.pallas import tpu as pltpu
from jax.sharding import PartitionSpec as P

D = 768
HDIM = 64
BLK = 128


def shifted(x, axis, by):
    size = lax.axis_size(axis)
    pairs = [(i, i + by) for i in range(size) if 0 <= i + by < size]
    return lax.ppermute(x, axis, pairs)


def gather_all(x, axis):
    size = lax.axis_size(axis)
    held = x[None]
    if size <= 8:
        got = [
            lax.ppermute(held, axis, [(i, (i + d) % size) for i in range(size)])
            for d in range(size - 1, 0, -1)
        ]
        return jnp.concatenate(got + [held], axis=0)
    step = 1
    while step < size:
        pairs = [(i, (i + step) % size) for i in range(size)]
        got = lax.ppermute(held, axis, pairs)
        held = jnp.concatenate([got, held], axis=0)
        step *= 2
    return held


def attention_kernel(count, source, rows, q_ref, *refs, heads, widths, scale):
    tables = refs[:-2]
    o_ref, kv_ref = refs[-2:]
    b = pl.program_id(0)
    used = count[b]

    @pl.when(b == 0)
    def _():
        kv_ref[...] = jnp.zeros_like(kv_ref)

    def fetch(j, carry):
        at = pl.multiple_of(j * BLK, BLK)
        row = rows[b, j]
        for code in range(len(tables)):
            @pl.when(source[b, j] == code)
            def _():
                start = pl.multiple_of(row * BLK, BLK)
                kv_ref[pl.ds(at, BLK), :] = tables[code][pl.ds(start, BLK), :]

        return carry

    lax.fori_loop(0, used, fetch, 0)
    limit = used * BLK

    width = heads * HDIM

    def run(slots):
        span = slots * BLK
        lane = lax.broadcasted_iota(jnp.int32, (1, span), 1)
        bias = jnp.where(lane < limit, 0.0, -jnp.inf)
        for h in range(heads):
            cols = slice(h * HDIM, (h + 1) * HDIM)
            qh = (q_ref[0, :, cols].astype(jnp.float32) * scale).astype(jnp.bfloat16)
            s = lax.dot_general(qh, kv_ref[0:span, cols], (((1,), (1,)), ((), ())),
                                preferred_element_type=jnp.float32) + bias
            peak = jnp.max(s, axis=-1, keepdims=True)
            e = jnp.exp(s - peak)
            totals = jnp.sum(e, axis=-1, keepdims=True)
            vcols = slice(width + h * HDIM, width + (h + 1) * HDIM)
            summed = jnp.dot(e.astype(jnp.bfloat16), kv_ref[0:span, vcols],
                             preferred_element_type=jnp.float32)
            o_ref[0, :, cols] = (summed / totals).astype(o_ref.dtype)

    low = 0
    for slots in widths:
        @pl.when((used > low) & (used <= slots))
        def _():
            run(slots)
        low = slots


def attention(queries, tables, count, source, rows, widths=None):
    block_count, _, width = queries.shape
    heads = width // HDIM
    slots = rows.shape[1]
    if widths is None:
        widths = tuple(w for w in (8, 12, 16) if w < slots) + (slots,)
    kernel = functools.partial(attention_kernel, heads=heads, widths=widths,
                               scale=HDIM ** (-0.5))
    whole = pl.BlockSpec(memory_space=pltpu.VMEM)
    keys = slots * BLK
    return pl.pallas_call(
        kernel,
        out_shape=jax.ShapeDtypeStruct(queries.shape, jnp.bfloat16),
        grid_spec=pltpu.PrefetchScalarGridSpec(
            num_scalar_prefetch=3,
            grid=(block_count,),
            in_specs=[
                pl.BlockSpec((1, BLK, width), lambda b, *_: (b, 0, 0)),
            ] + [whole] * len(tables),
            out_specs=pl.BlockSpec((1, BLK, width), lambda b, *_: (b, 0, 0)),
            scratch_shapes=[
                pltpu.VMEM((keys, 2 * width), jnp.bfloat16),
            ],
        ),
        compiler_params=pltpu.CompilerParams(vmem_limit_bytes=60 * 1024 * 1024),
        cost_estimate=pl.CostEstimate(
            flops=4 * block_count * BLK * keys * width,
            transcendentals=block_count * heads * BLK * keys,
            bytes_accessed=sum(t.size * t.dtype.itemsize for t in tables) + 2 * queries.size * 2,
        ),
    )(count, source, rows, queries, *tables)


def project_kv(x, kv_w):
    return jnp.dot(x, kv_w, preferred_element_type=jnp.float32).astype(jnp.bfloat16)


def window_of(x, axis):
    parts = []
    for offset in (2, 1, 0, -1, -2):
        parts.append(x if offset == 0 else shifted(x, "seq", offset))
    return jnp.concatenate(parts, axis=axis)


def shards(tokens, w_qkv, w_out, neighbours, near_count, anchors):
    head_count = lax.axis_size("head")
    head_rank = lax.axis_index("head")
    width_here = D // head_count
    own_rows = tokens.shape[0]
    own_blocks = own_rows // BLK
    row_count = own_rows * head_count
    block_count = row_count // BLK
    neigh = neighbours.shape[1]
    col_start = head_rank * width_here
    query_w = lax.dynamic_slice_in_dim(w_qkv[:, 0], col_start, width_here, 1)
    key_w = lax.dynamic_slice_in_dim(w_qkv[:, 1], col_start, width_here, 1)
    value_w = lax.dynamic_slice_in_dim(w_qkv[:, 2], col_start, width_here, 1)

    kv_w = jnp.concatenate([key_w, value_w], axis=1)
    kva = window_of(project_kv(tokens, kv_w), 0)

    def fetch_chunk(source, k):
        pairs = [(z, (z - k) % head_count) for z in range(head_count)]
        return lax.ppermute(source, "head", pairs)

    near_k = sorted({1, head_count - 1})
    groups = [near_k] + ([[k for k in range(1, head_count) if k not in near_k]]
                         if head_count > 3 else [])
    group_of, slot_of, size_of = [0] * head_count, [0] * head_count, [0] * head_count
    kv_groups = []
    received = {}
    source = tokens
    for g, members in enumerate(groups):
        for p, k in enumerate(members):
            group_of[k], slot_of[k], size_of[k] = g, p, len(members)
            received[k] = fetch_chunk(source, k)
        kv = project_kv(jnp.concatenate([received[k] for k in members], axis=0), kv_w)
        source, kv = lax.optimization_barrier((tokens, kv))
        kv_groups.append(window_of(kv, 0))
    rest_tokens = jnp.concatenate([received[k] for k in range(1, head_count)], axis=0)
    rolled_tokens = jnp.concatenate([tokens, rest_tokens], axis=0)
    queries = jnp.dot(rolled_tokens, query_w, preferred_element_type=jnp.float32).astype(
        jnp.bfloat16
    ).reshape(block_count, BLK, width_here)

    seq_count = lax.axis_size("seq")
    seq_rank = lax.axis_index("seq")
    late = [k for members in groups[1:] for k in members]
    first_hop = (-head_rank) % head_count
    first_rows = tokens[:BLK]
    if late:
        early_first = lax.ppermute(tokens[:BLK], "head",
                                   [(0, (-k) % head_count) for k in late])
        for k in late:
            first_rows = jnp.where(first_hop == k, early_first, first_rows)
    for k in groups[0]:
        first_rows = jnp.where(first_hop == k, received[k][:BLK], first_rows)
    kvanc = gather_all(project_kv(first_rows, kv_w), "seq")
    held_count = kvanc.shape[0]
    kvanc = kvanc.reshape(held_count * BLK, 2 * width_here)
    first_block = (seq_rank - 2) * block_count

    shift = -head_rank * own_blocks
    neighbours = jnp.roll(neighbours, shift, axis=0)
    near_count = jnp.roll(near_count, shift, axis=0)
    anchors = jnp.roll(anchors, shift, axis=0)

    rel = jnp.clip(neighbours - first_block, 0, 5 * block_count - 1)
    offset_idx = rel // block_count
    within = rel % block_count
    chunk = within // own_blocks
    inner = within % own_blocks
    mine = chunk == head_rank
    row_a = offset_idx * own_blocks + inner
    hop = (chunk - head_rank) % head_count
    hop_group = jnp.asarray(group_of, jnp.int32)[hop]
    hop_slot = jnp.asarray(slot_of, jnp.int32)[hop]
    hop_size = jnp.asarray(size_of, jnp.int32)[hop]
    row_b = (offset_idx * hop_size + hop_slot) * own_blocks + inner
    near_row = jnp.where(mine, row_a, row_b)
    near_src = jnp.where(mine, 0, 1 + hop_group)
    owner = jnp.clip(anchors // block_count, 0, seq_count - 1)
    anch_row = (owner - seq_rank + held_count - 1) % seq_count
    near_used = jnp.arange(neigh)[None, :] < near_count[:, None]
    repeated = jnp.any(
        (anchors[:, :, None] == neighbours[:, None, :]) & near_used[:, None, :], axis=2
    )
    valid = jnp.concatenate([near_used, jnp.logical_not(repeated)], axis=1)
    order = jnp.argsort(jnp.logical_not(valid).astype(jnp.int32), axis=1, stable=True)
    every_row = jnp.concatenate([near_row, anch_row], axis=1)
    every_src = jnp.concatenate([near_src, jnp.full_like(anch_row, 1 + len(groups))], axis=1)
    rows = jnp.take_along_axis(every_row, order, axis=1).astype(jnp.int32)
    source = jnp.take_along_axis(every_src, order, axis=1).astype(jnp.int32)
    count = jnp.sum(valid.astype(jnp.int32), axis=1).astype(jnp.int32)

    tables = (kva, *kv_groups, kvanc)
    away = attention(queries[own_blocks:], tables, count[own_blocks:], source[own_blocks:],
                     rows[own_blocks:])
    away = away.reshape(head_count - 1, own_rows, width_here)
    received = [None] * head_count
    for j in range(1, head_count):
        pairs = [(z, (z + j) % head_count) for z in range(head_count)]
        received[j] = lax.ppermute(away[j - 1], "head", pairs)
    received[0] = attention(queries[:own_blocks], tables, count[:own_blocks],
                            source[:own_blocks], rows[:own_blocks]).reshape(own_rows, width_here)
    mine_rows = jnp.concatenate(received, axis=1)
    groups = (head_rank - jnp.arange(head_count)) % head_count
    out_w = jnp.take(w_out.reshape(head_count, width_here, D), groups, axis=0).reshape(D, D)
    mixed_out = jnp.dot(mine_rows, out_w, preferred_element_type=jnp.float32).astype(
        jnp.bfloat16
    )
    return mixed_out


def solution(mesh):
    placed = (P(("seq", "head"), None), P(), P(), P("seq", None), P("seq"), P("seq", None))
    return jax.shard_map(
        shards, mesh=mesh, in_specs=placed, out_specs=P(("seq", "head"), None), check_vma=False
    )
```

```python
import functools

import jax
import jax.numpy as jnp
from jax import lax
from jax.experimental import pallas as pl
from jax.experimental.pallas import tpu as pltpu
from jax.sharding import PartitionSpec as P

D = 768
HDIM = 64
BLK = 128


def shifted(x, axis, by):
    size = lax.axis_size(axis)
    pairs = [(i, i + by) for i in range(size) if 0 <= i + by < size]
    return lax.ppermute(x, axis, pairs)


def gather_all(x, axis):
    size = lax.axis_size(axis)
    held = x[None]
    if size <= 8:
        got = [
            lax.ppermute(held, axis, [(i, (i + d) % size) for i in range(size)])
            for d in range(size - 1, 0, -1)
        ]
        return jnp.concatenate(got + [held], axis=0)
    step = 1
    while step < size:
        pairs = [(i, (i + step) % size) for i in range(size)]
        got = lax.ppermute(held, axis, pairs)
        held = jnp.concatenate([got, held], axis=0)
        step *= 2
    return held


def attention_kernel(count, source, rows, q_ref, *refs, heads, widths, scale):
    tables = refs[:-2]
    o_ref, kv_ref = refs[-2:]
    b = pl.program_id(0)
    used = count[b]

    @pl.when(b == 0)
    def _():
        kv_ref[...] = jnp.zeros_like(kv_ref)

    def fetch(j, carry):
        at = pl.multiple_of(j * BLK, BLK)
        row = rows[b, j]
        for code in range(len(tables)):
            @pl.when(source[b, j] == code)
            def _():
                start = pl.multiple_of(row * BLK, BLK)
                kv_ref[pl.ds(at, BLK), :] = tables[code][pl.ds(start, BLK), :]

        return carry

    lax.fori_loop(0, used, fetch, 0)
    limit = used * BLK

    width = heads * HDIM

    def run(slots):
        span = slots * BLK
        lane = lax.broadcasted_iota(jnp.int32, (1, span), 1)
        bias = jnp.where(lane < limit, 0.0, -jnp.inf)
        for h in range(heads):
            cols = slice(h * HDIM, (h + 1) * HDIM)
            qh = (q_ref[0, :, cols].astype(jnp.float32) * scale).astype(jnp.bfloat16)
            s = lax.dot_general(qh, kv_ref[0:span, cols], (((1,), (1,)), ((), ())),
                                preferred_element_type=jnp.float32) + bias
            peak = jnp.max(s, axis=-1, keepdims=True)
            e = jnp.exp(s - peak)
            totals = jnp.sum(e, axis=-1, keepdims=True)
            vcols = slice(width + h * HDIM, width + (h + 1) * HDIM)
            summed = jnp.dot(e.astype(jnp.bfloat16), kv_ref[0:span, vcols],
                             preferred_element_type=jnp.float32)
            o_ref[0, :, cols] = (summed / totals).astype(o_ref.dtype)

    low = 0
    for slots in widths:
        @pl.when((used > low) & (used <= slots))
        def _():
            run(slots)
        low = slots


def attention(queries, tables, count, source, rows, widths=None):
    block_count, _, width = queries.shape
    heads = width // HDIM
    slots = rows.shape[1]
    if widths is None:
        widths = tuple(w for w in (8, 12, 16) if w < slots) + (slots,)
    kernel = functools.partial(attention_kernel, heads=heads, widths=widths,
                               scale=HDIM ** (-0.5))
    whole = pl.BlockSpec(memory_space=pltpu.VMEM)
    keys = slots * BLK
    return pl.pallas_call(
        kernel,
        out_shape=jax.ShapeDtypeStruct(queries.shape, jnp.bfloat16),
        grid_spec=pltpu.PrefetchScalarGridSpec(
            num_scalar_prefetch=3,
            grid=(block_count,),
            in_specs=[
                pl.BlockSpec((1, BLK, width), lambda b, *_: (b, 0, 0)),
            ] + [whole] * len(tables),
            out_specs=pl.BlockSpec((1, BLK, width), lambda b, *_: (b, 0, 0)),
            scratch_shapes=[
                pltpu.VMEM((keys, 2 * width), jnp.bfloat16),
            ],
        ),
        compiler_params=pltpu.CompilerParams(vmem_limit_bytes=60 * 1024 * 1024),
        cost_estimate=pl.CostEstimate(
            flops=4 * block_count * BLK * keys * width,
            transcendentals=block_count * heads * BLK * keys,
            bytes_accessed=sum(t.size * t.dtype.itemsize for t in tables) + 2 * queries.size * 2,
        ),
    )(count, source, rows, queries, *tables)


def project_kv(x, kv_w):
    return jnp.dot(x, kv_w, preferred_element_type=jnp.float32).astype(jnp.bfloat16)


def window_of(x, axis):
    parts = []
    for offset in (2, 1, 0, -1, -2):
        parts.append(x if offset == 0 else shifted(x, "seq", offset))
    return jnp.concatenate(parts, axis=axis)


def shards(tokens, w_qkv, w_out, neighbours, near_count, anchors):
    head_count = lax.axis_size("head")
    head_rank = lax.axis_index("head")
    width_here = D // head_count
    own_rows = tokens.shape[0]
    own_blocks = own_rows // BLK
    row_count = own_rows * head_count
    block_count = row_count // BLK
    neigh = neighbours.shape[1]
    col_start = head_rank * width_here
    query_w = lax.dynamic_slice_in_dim(w_qkv[:, 0], col_start, width_here, 1)
    key_w = lax.dynamic_slice_in_dim(w_qkv[:, 1], col_start, width_here, 1)
    value_w = lax.dynamic_slice_in_dim(w_qkv[:, 2], col_start, width_here, 1)

    kv_w = jnp.concatenate([key_w, value_w], axis=1)
    kva = window_of(project_kv(tokens, kv_w), 0)

    def fetch_chunk(source, k):
        pairs = [(z, (z - k) % head_count) for z in range(head_count)]
        return lax.ppermute(source, "head", pairs)

    near_k = sorted({1, head_count - 1})
    groups = [near_k] + ([[k for k in range(1, head_count) if k not in near_k]]
                         if head_count > 3 else [])
    group_of, slot_of, size_of = [0] * head_count, [0] * head_count, [0] * head_count
    kv_groups = []
    received = {}
    source = tokens
    for g, members in enumerate(groups):
        for p, k in enumerate(members):
            group_of[k], slot_of[k], size_of[k] = g, p, len(members)
            received[k] = fetch_chunk(source, k)
        kv = project_kv(jnp.concatenate([received[k] for k in members], axis=0), kv_w)
        source, kv = lax.optimization_barrier((tokens, kv))
        kv_groups.append(window_of(kv, 0))
    rest_tokens = jnp.concatenate([received[k] for k in range(1, head_count)], axis=0)
    rolled_tokens = jnp.concatenate([tokens, rest_tokens], axis=0)
    queries = jnp.dot(rolled_tokens, query_w, preferred_element_type=jnp.float32).astype(
        jnp.bfloat16
    ).reshape(block_count, BLK, width_here)

    seq_count = lax.axis_size("seq")
    seq_rank = lax.axis_index("seq")
    first_at = ((head_count - head_rank) % head_count) * own_rows
    first_rows = lax.dynamic_slice_in_dim(rolled_tokens, first_at, BLK, 0)
    kvanc = gather_all(project_kv(first_rows, kv_w), "seq")
    held_count = kvanc.shape[0]
    kvanc = kvanc.reshape(held_count * BLK, 2 * width_here)
    first_block = (seq_rank - 2) * block_count

    shift = -head_rank * own_blocks
    neighbours = jnp.roll(neighbours, shift, axis=0)
    near_count = jnp.roll(near_count, shift, axis=0)
    anchors = jnp.roll(anchors, shift, axis=0)

    rel = jnp.clip(neighbours - first_block, 0, 5 * block_count - 1)
    offset_idx = rel // block_count
    within = rel % block_count
    chunk = within // own_blocks
    inner = within % own_blocks
    mine = chunk == head_rank
    row_a = offset_idx * own_blocks + inner
    hop = (chunk - head_rank) % head_count
    hop_group = jnp.asarray(group_of, jnp.int32)[hop]
    hop_slot = jnp.asarray(slot_of, jnp.int32)[hop]
    hop_size = jnp.asarray(size_of, jnp.int32)[hop]
    row_b = (offset_idx * hop_size + hop_slot) * own_blocks + inner
    near_row = jnp.where(mine, row_a, row_b)
    near_src = jnp.where(mine, 0, 1 + hop_group)
    owner = jnp.clip(anchors // block_count, 0, seq_count - 1)
    anch_row = (owner - seq_rank + held_count - 1) % seq_count
    near_used = jnp.arange(neigh)[None, :] < near_count[:, None]
    repeated = jnp.any(
        (anchors[:, :, None] == neighbours[:, None, :]) & near_used[:, None, :], axis=2
    )
    valid = jnp.concatenate([near_used, jnp.logical_not(repeated)], axis=1)
    order = jnp.argsort(jnp.logical_not(valid).astype(jnp.int32), axis=1, stable=True)
    every_row = jnp.concatenate([near_row, anch_row], axis=1)
    every_src = jnp.concatenate([near_src, jnp.full_like(anch_row, 1 + len(groups))], axis=1)
    rows = jnp.take_along_axis(every_row, order, axis=1).astype(jnp.int32)
    source = jnp.take_along_axis(every_src, order, axis=1).astype(jnp.int32)
    count = jnp.sum(valid.astype(jnp.int32), axis=1).astype(jnp.int32)

    tables = (kva, *kv_groups, kvanc)
    away = attention(queries[own_blocks:], tables, count[own_blocks:], source[own_blocks:],
                     rows[own_blocks:])
    away = away.reshape(head_count - 1, own_rows, width_here)
    received = [None] * head_count
    for j in range(1, head_count):
        pairs = [(z, (z + j) % head_count) for z in range(head_count)]
        received[j] = lax.ppermute(away[j - 1], "head", pairs)
    received[0] = attention(queries[:own_blocks], tables, count[:own_blocks],
                            source[:own_blocks], rows[:own_blocks]).reshape(own_rows, width_here)
    mine_rows = jnp.concatenate(received, axis=1)
    groups = (head_rank - jnp.arange(head_count)) % head_count
    out_w = jnp.take(w_out.reshape(head_count, width_here, D), groups, axis=0).reshape(D, D)
    mixed_out = jnp.dot(mine_rows, out_w, preferred_element_type=jnp.float32).astype(
        jnp.bfloat16
    )
    return mixed_out


def solution(mesh):
    placed = (P(("seq", "head"), None), P(), P(), P("seq", None), P("seq"), P("seq", None))
    return jax.shard_map(
        shards, mesh=mesh, in_specs=placed, out_specs=P(("seq", "head"), None), check_vma=False
    )
```

```python
import functools

import jax
import jax.numpy as jnp
from jax import lax
from jax.experimental import pallas as pl
from jax.experimental.pallas import tpu as pltpu
from jax.sharding import PartitionSpec as P

D = 768
HDIM = 64
BLK = 128


def shifted(x, axis, by):
    size = lax.axis_size(axis)
    pairs = [(i, i + by) for i in range(size) if 0 <= i + by < size]
    return lax.ppermute(x, axis, pairs)


def gather_all(x, axis):
    size = lax.axis_size(axis)
    held = x[None]
    if size <= 8:
        got = [
            lax.ppermute(held, axis, [(i, (i + d) % size) for i in range(size)])
            for d in range(size - 1, 0, -1)
        ]
        return jnp.concatenate(got + [held], axis=0)
    step = 1
    while step < size:
        pairs = [(i, (i + step) % size) for i in range(size)]
        got = lax.ppermute(held, axis, pairs)
        held = jnp.concatenate([got, held], axis=0)
        step *= 2
    return held


def attention_kernel(count, source, rows, q_ref, *refs, heads, widths, scale):
    tables = refs[:-2]
    o_ref, kv_ref = refs[-2:]
    b = pl.program_id(0)
    used = count[b]

    @pl.when(b == 0)
    def _():
        kv_ref[...] = jnp.zeros_like(kv_ref)

    def fetch(j, carry):
        at = pl.multiple_of(j * BLK, BLK)
        row = rows[b, j]
        for code in range(len(tables)):
            @pl.when(source[b, j] == code)
            def _():
                start = pl.multiple_of(row * BLK, BLK)
                kv_ref[pl.ds(at, BLK), :] = tables[code][pl.ds(start, BLK), :]

        return carry

    lax.fori_loop(0, used, fetch, 0)
    limit = used * BLK

    width = heads * HDIM

    def run(slots):
        span = slots * BLK
        lane = lax.broadcasted_iota(jnp.int32, (1, span), 1)
        bias = jnp.where(lane < limit, 0.0, -jnp.inf)
        for h in range(heads):
            cols = slice(h * HDIM, (h + 1) * HDIM)
            qh = (q_ref[0, :, cols].astype(jnp.float32) * scale).astype(jnp.bfloat16)
            s = lax.dot_general(qh, kv_ref[0:span, cols], (((1,), (1,)), ((), ())),
                                preferred_element_type=jnp.float32) + bias
            peak = jnp.max(s, axis=-1, keepdims=True)
            e = jnp.exp(s - peak)
            totals = jnp.sum(e, axis=-1, keepdims=True)
            vcols = slice(width + h * HDIM, width + (h + 1) * HDIM)
            summed = jnp.dot(e.astype(jnp.bfloat16), kv_ref[0:span, vcols],
                             preferred_element_type=jnp.float32)
            o_ref[0, :, cols] = (summed / totals).astype(o_ref.dtype)

    low = 0
    for slots in widths:
        @pl.when((used > low) & (used <= slots))
        def _():
            run(slots)
        low = slots


def attention(queries, tables, count, source, rows, widths=None):
    block_count, _, width = queries.shape
    heads = width // HDIM
    slots = rows.shape[1]
    if widths is None:
        widths = tuple(w for w in (8, 10, 12, 14, 16, 18) if w < slots) + (slots,)
    kernel = functools.partial(attention_kernel, heads=heads, widths=widths,
                               scale=HDIM ** (-0.5))
    whole = pl.BlockSpec(memory_space=pltpu.VMEM)
    keys = slots * BLK
    return pl.pallas_call(
        kernel,
        out_shape=jax.ShapeDtypeStruct(queries.shape, jnp.bfloat16),
        grid_spec=pltpu.PrefetchScalarGridSpec(
            num_scalar_prefetch=3,
            grid=(block_count,),
            in_specs=[
                pl.BlockSpec((1, BLK, width), lambda b, *_: (b, 0, 0)),
            ] + [whole] * len(tables),
            out_specs=pl.BlockSpec((1, BLK, width), lambda b, *_: (b, 0, 0)),
            scratch_shapes=[
                pltpu.VMEM((keys, 2 * width), jnp.bfloat16),
            ],
        ),
        compiler_params=pltpu.CompilerParams(vmem_limit_bytes=60 * 1024 * 1024),
        cost_estimate=pl.CostEstimate(
            flops=4 * block_count * BLK * keys * width,
            transcendentals=block_count * heads * BLK * keys,
            bytes_accessed=sum(t.size * t.dtype.itemsize for t in tables) + 2 * queries.size * 2,
        ),
    )(count, source, rows, queries, *tables)


def project_kv(x, kv_w):
    return jnp.dot(x, kv_w, preferred_element_type=jnp.float32).astype(jnp.bfloat16)


def window_of(x, axis):
    parts = []
    for offset in (2, 1, 0, -1, -2):
        parts.append(x if offset == 0 else shifted(x, "seq", offset))
    return jnp.concatenate(parts, axis=axis)


def shards(tokens, w_qkv, w_out, neighbours, near_count, anchors):
    head_count = lax.axis_size("head")
    head_rank = lax.axis_index("head")
    width_here = D // head_count
    own_rows = tokens.shape[0]
    own_blocks = own_rows // BLK
    row_count = own_rows * head_count
    block_count = row_count // BLK
    neigh = neighbours.shape[1]
    col_start = head_rank * width_here
    query_w = lax.dynamic_slice_in_dim(w_qkv[:, 0], col_start, width_here, 1)
    key_w = lax.dynamic_slice_in_dim(w_qkv[:, 1], col_start, width_here, 1)
    value_w = lax.dynamic_slice_in_dim(w_qkv[:, 2], col_start, width_here, 1)

    kv_w = jnp.concatenate([key_w, value_w], axis=1)
    kva = window_of(project_kv(tokens, kv_w), 0)

    def fetch_chunk(source, k):
        pairs = [(z, (z - k) % head_count) for z in range(head_count)]
        return lax.ppermute(source, "head", pairs)

    near_k = sorted({1, head_count - 1})
    groups = [near_k] + ([[k for k in range(1, head_count) if k not in near_k]]
                         if head_count > 3 else [])
    group_of, slot_of, size_of = [0] * head_count, [0] * head_count, [0] * head_count
    kv_groups = []
    received = {}
    source = tokens
    for g, members in enumerate(groups):
        for p, k in enumerate(members):
            group_of[k], slot_of[k], size_of[k] = g, p, len(members)
            received[k] = fetch_chunk(source, k)
        kv = project_kv(jnp.concatenate([received[k] for k in members], axis=0), kv_w)
        source, kv = lax.optimization_barrier((tokens, kv))
        kv_groups.append(window_of(kv, 0))
    rest_tokens = jnp.concatenate([received[k] for k in range(1, head_count)], axis=0)
    rolled_tokens = jnp.concatenate([tokens, rest_tokens], axis=0)
    queries = jnp.dot(rolled_tokens, query_w, preferred_element_type=jnp.float32).astype(
        jnp.bfloat16
    ).reshape(block_count, BLK, width_here)

    seq_count = lax.axis_size("seq")
    seq_rank = lax.axis_index("seq")
    first_at = ((head_count - head_rank) % head_count) * own_rows
    first_rows = lax.dynamic_slice_in_dim(rolled_tokens, first_at, BLK, 0)
    kvanc = gather_all(project_kv(first_rows, kv_w), "seq")
    held_count = kvanc.shape[0]
    kvanc = kvanc.reshape(held_count * BLK, 2 * width_here)
    first_block = (seq_rank - 2) * block_count

    shift = -head_rank * own_blocks
    neighbours = jnp.roll(neighbours, shift, axis=0)
    near_count = jnp.roll(near_count, shift, axis=0)
    anchors = jnp.roll(anchors, shift, axis=0)

    rel = jnp.clip(neighbours - first_block, 0, 5 * block_count - 1)
    offset_idx = rel // block_count
    within = rel % block_count
    chunk = within // own_blocks
    inner = within % own_blocks
    mine = chunk == head_rank
    row_a = offset_idx * own_blocks + inner
    hop = (chunk - head_rank) % head_count
    hop_group = jnp.asarray(group_of, jnp.int32)[hop]
    hop_slot = jnp.asarray(slot_of, jnp.int32)[hop]
    hop_size = jnp.asarray(size_of, jnp.int32)[hop]
    row_b = (offset_idx * hop_size + hop_slot) * own_blocks + inner
    near_row = jnp.where(mine, row_a, row_b)
    near_src = jnp.where(mine, 0, 1 + hop_group)
    owner = jnp.clip(anchors // block_count, 0, seq_count - 1)
    anch_row = (owner - seq_rank + held_count - 1) % seq_count
    near_used = jnp.arange(neigh)[None, :] < near_count[:, None]
    repeated = jnp.any(
        (anchors[:, :, None] == neighbours[:, None, :]) & near_used[:, None, :], axis=2
    )
    valid = jnp.concatenate([near_used, jnp.logical_not(repeated)], axis=1)
    order = jnp.argsort(jnp.logical_not(valid).astype(jnp.int32), axis=1, stable=True)
    every_row = jnp.concatenate([near_row, anch_row], axis=1)
    every_src = jnp.concatenate([near_src, jnp.full_like(anch_row, 1 + len(groups))], axis=1)
    rows = jnp.take_along_axis(every_row, order, axis=1).astype(jnp.int32)
    source = jnp.take_along_axis(every_src, order, axis=1).astype(jnp.int32)
    count = jnp.sum(valid.astype(jnp.int32), axis=1).astype(jnp.int32)

    tables = (kva, *kv_groups, kvanc)
    away = attention(queries[own_blocks:], tables, count[own_blocks:], source[own_blocks:],
                     rows[own_blocks:])
    away = away.reshape(head_count - 1, own_rows, width_here)
    received = [None] * head_count
    for j in range(1, head_count):
        pairs = [(z, (z + j) % head_count) for z in range(head_count)]
        received[j] = lax.ppermute(away[j - 1], "head", pairs)
    received[0] = attention(queries[:own_blocks], tables, count[:own_blocks],
                            source[:own_blocks], rows[:own_blocks]).reshape(own_rows, width_here)
    mine_rows = jnp.concatenate(received, axis=1)
    groups = (head_rank - jnp.arange(head_count)) % head_count
    out_w = jnp.take(w_out.reshape(head_count, width_here, D), groups, axis=0).reshape(D, D)
    mixed_out = jnp.dot(mine_rows, out_w, preferred_element_type=jnp.float32).astype(
        jnp.bfloat16
    )
    return mixed_out


def solution(mesh):
    placed = (P(("seq", "head"), None), P(), P(), P("seq", None), P("seq"), P("seq", None))
    return jax.shard_map(
        shards, mesh=mesh, in_specs=placed, out_specs=P(("seq", "head"), None), check_vma=False
    )
```
